256 devices in a mesh: sample: 32 (over x, y, core), slab: 8 (over z).
Axes of the slice: x: 4, y: 4, z: 8, core: 2. Of those that a mesh axis runs over, the one named last changes fastest.
Arguments:
- volume: bfloat16 [4, 32, 32, 4096], P(None, 'sample', 'slab'), may hold values from -6 to 6
- cotangent: bfloat16 [128, 32, 8, 256], P(None, 'sample', 'slab'), may hold values from -0.5 to 0.5
- w_first: bfloat16 [27, 4, 32], replicated, may hold values from -0.625 to 0.625
- b_first: float32 [32], replicated, may hold values from -3 to 3
- w_second: bfloat16 [27, 32, 64], replicated, may hold values from -0.21875 to 0.21875
- b_second: float32 [64], replicated, may hold values from -3 to 3
- w_third: bfloat16 [27, 64, 128], replicated, may hold values from -0.15625 to 0.15625
- b_third: float32 [128], replicated, may hold values from -3 to 3
Outputs:
- features: bfloat16 [128, 32, 8, 256], P(None, 'sample', 'slab')
- kernel_grad_first: float32 [27, 4, 32], replicated
- bias_grad_first: float32 [32], replicated
- kernel_grad_second: float32 [27, 32, 64], replicated
- bias_grad_second: float32 [64], replicated
- kernel_grad_third: float32 [27, 64, 128], replicated
- bias_grad_third: float32 [128], replicated
The draws below stay inside these ranges and needn't reach their ends.
All inputs are finite; a program needn't handle non-finite values.
Results may differ from the reference program's by a relative error of at most 0.02.
Values may be sent and summed in bfloat16 or wider, within the bound.
No kernel may reach another device: no remote copies, remote signals or barrier semaphores. Data moves between devices by JAX's collectives and lax.ppermute only.
A program may use at most 128 MiB of HBM per device.

```python
import jax
import jax.numpy as jnp
from jax import lax

C0 = 4
C1 = 32
C2 = 64
C3 = 128
SX = 32
SY = 128
BATCH = 32
NZ = 32


def steps_of(stream_key, extent, pieces, low, high):
    level, own = 1.0, jax.random.fold_in(stream_key, 6)
    for dim, blocks in pieces:
        steps = jnp.exp(jax.random.uniform(jax.random.fold_in(own, dim), (blocks,), jnp.float32, low / len(pieces), high / len(pieces)))
        level = level * jnp.repeat(steps, extent[dim] // blocks).reshape([-1 if axis == dim else 1 for axis in range(len(extent))])
    return level


def bell_draw(stream_key, dims, width, most, pieces=(), kind=jnp.bfloat16):
    entries = jax.random.normal(stream_key, dims, jnp.float32) * width
    if len(pieces) > 0:
        entries = steps_of(stream_key, dims, pieces, -0.22, 0.18) * entries
    return jnp.clip(entries, min=-most, max=most).astype(kind)


def setup_inputs(seed: int = 0) -> dict:
    arg_keys = jax.random.split(jax.random.key(seed), 9)
    volume = bell_draw(arg_keys[0], (C0, BATCH, NZ, SY * SX), 1.0, 6.0, ((1, 32), (2, 8)))
    cotangent = bell_draw(arg_keys[1], (C3, BATCH, NZ // 4, SY * SX // 16), (8.0 / (BATCH * NZ * SX * SY // 64) ** 0.5), 0.5, ((1, 32), (2, 8)))
    w_first = bell_draw(arg_keys[2], (27, C0, C1), (27 * C0) ** -0.5, 0.625)
    b_first = bell_draw(arg_keys[3], (C1,), 0.5, 3.0, (), jnp.float32)
    w_second = bell_draw(arg_keys[4], (27, C1, C2), (27 * C1) ** -0.5, 0.21875)
    b_second = bell_draw(arg_keys[5], (C2,), 0.5, 3.0, (), jnp.float32)
    w_third = bell_draw(arg_keys[6], (27, C2, C3), (27 * C2) ** -0.5, 0.15625)
    b_third = bell_draw(arg_keys[7], (C3,), 0.5, 3.0, (), jnp.float32)
    return dict(volume=volume, cotangent=cotangent, w_first=w_first, b_first=b_first, w_second=w_second, b_second=b_second, w_third=w_third, b_third=b_third)


def silu_slope(values):
    sigmoid = jax.nn.sigmoid(values)
    return sigmoid * (1.0 + values * (1.0 - sigmoid))


def shifted_views(source):
    padded = jnp.pad(source, ((0, 0), (1, 1), (1, 1), (1, 1)))
    depth_len, row_count, row_width = source.shape[1], source.shape[2], source.shape[3]
    shifted = []
    for tap_index in range(27):
        depth_start = tap_index // 9
        row_start = tap_index // 3 % 3
        column_start = tap_index % 3
        shifted.append(padded[:, depth_start:depth_start + depth_len, row_start:row_start + row_count, column_start:column_start + row_width])
    return shifted


def convolve(source, weight):
    summed = jnp.zeros((weight.shape[2],) + source.shape[1:], jnp.float32)
    for tap_index, shifted in enumerate(shifted_views(source)):
        summed = summed + jnp.einsum('izyx,io->ozyx', shifted.astype(jnp.float32), weight[tap_index].astype(jnp.float32))
    return summed


def weight_sums(source, delta_values):
    grads = delta_values.astype(jnp.float32)
    return jnp.stack([jnp.einsum('izyx,ozyx->io', shifted.astype(jnp.float32), grads) for shifted in shifted_views(source)])


def pool_cells(values):
    channels, depth_len, row_count, row_width = values.shape
    grouped = values.reshape(channels, depth_len // 2, 2, row_count // 2, 2, row_width // 2, 2)
    return grouped.mean(axis=(2, 4, 6))


def spread_cells(values):
    widened = jnp.repeat(jnp.repeat(jnp.repeat(values, 2, axis=1), 2, axis=2), 2, axis=3)
    return widened * 0.125


def reference(volume, cotangent, w_first, b_first, w_second, b_second, w_third, b_third):
    flipped_second = jnp.flip(w_second, 0).transpose(0, 2, 1)
    flipped_third = jnp.flip(w_third, 0).transpose(0, 2, 1)

    def per_sample(totals, sample):
        source = lax.dynamic_index_in_dim(volume, sample, 1, keepdims=False).reshape(C0, NZ, SY, SX)
        upstream = lax.dynamic_index_in_dim(cotangent, sample, 1, keepdims=False).reshape(C3, NZ // 4, SY // 4, SX // 4)
        first_pre = (convolve(source, w_first) + b_first[:, None, None, None]).astype(jnp.bfloat16)
        first_pooled = pool_cells(jax.nn.silu(first_pre.astype(jnp.float32))).astype(jnp.bfloat16)
        second_pre = (convolve(first_pooled, w_second) + b_second[:, None, None, None]).astype(jnp.bfloat16)
        second_pooled = pool_cells(jax.nn.silu(second_pre.astype(jnp.float32))).astype(jnp.bfloat16)
        third_pre = (convolve(second_pooled, w_third) + b_third[:, None, None, None]).astype(jnp.bfloat16)
        features = jax.nn.silu(third_pre.astype(jnp.float32)).astype(jnp.bfloat16)
        third_delta = (upstream.astype(jnp.float32) * silu_slope(third_pre.astype(jnp.float32))).astype(jnp.bfloat16)
        second_back = convolve(third_delta, flipped_third).astype(jnp.bfloat16)
        second_delta = (spread_cells(second_back.astype(jnp.float32)) * silu_slope(second_pre.astype(jnp.float32))).astype(jnp.bfloat16)
        first_back = convolve(second_delta, flipped_second).astype(jnp.bfloat16)
        first_delta = (spread_cells(first_back.astype(jnp.float32)) * silu_slope(first_pre.astype(jnp.float32))).astype(jnp.bfloat16)
        contribution = (
            weight_sums(source, first_delta),
            jnp.sum(first_delta.astype(jnp.float32), axis=(1, 2, 3)),
            weight_sums(first_pooled, second_delta),
            jnp.sum(second_delta.astype(jnp.float32), axis=(1, 2, 3)),
            weight_sums(second_pooled, third_delta),
            jnp.sum(third_delta.astype(jnp.float32), axis=(1, 2, 3)),
        )
        totals = jax.tree.map(jnp.add, totals, contribution)
        return totals, features.reshape(C3, NZ // 4, SY * SX // 16)

    initial = (
        jnp.zeros((27, C0, C1), jnp.float32),
        jnp.zeros((C1,), jnp.float32),
        jnp.zeros((27, C1, C2), jnp.float32),
        jnp.zeros((C2,), jnp.float32),
        jnp.zeros((27, C2, C3), jnp.float32),
        jnp.zeros((C3,), jnp.float32),
    )
    totals, stacked = lax.scan(per_sample, initial, jnp.arange(BATCH, dtype=jnp.int32))
    features = jnp.transpose(stacked, (1, 0, 2, 3))
    return (features, totals[0], totals[1], totals[2], totals[3], totals[4], totals[5])
```

```python
import jax
import jax.numpy as jnp
from jax import lax
from jax.sharding import PartitionSpec as P

SX = 32
CZ = 4


def with_halo(shard, sides, width):
    for axis, dim in sides:
        size, length = (lax.axis_size(axis), shard.shape[dim])
        up = [(i, (i + 1) % size) for i in range(size - 1)]
        down = [(j, i) for i, j in up]
        last = lax.slice_in_dim(shard, length - width, length, axis=dim)
        first = lax.slice_in_dim(shard, 0, width, axis=dim)
        before = lax.ppermute(last, axis, up)
        after = lax.ppermute(first, axis, down)
        shard = jnp.concatenate([before, shard, after], axis=dim)
    return shard


def silu_slope(values):
    sigmoid = jax.nn.sigmoid(values)
    return sigmoid * (1.0 + values * (1.0 - sigmoid))


def put_block(values, update, sample, depth_start):
    return lax.dynamic_update_slice(values, update, (0, sample, depth_start, 0))


def gather_taps(section, row_width):
    depth_len = section.shape[2] - 2
    plane_size = section.shape[3]
    flattened = jnp.pad(section, ((0, 0), (0, 0), (0, 0), (row_width + 1, row_width + 1)))
    column = lax.broadcasted_iota(jnp.int32, (1, 1, 1, plane_size), 3) % row_width
    left_mask = (column >= 1).astype(section.dtype)
    right_mask = (column <= row_width - 2).astype(section.dtype)
    pieces = []
    for tap_index in range(27):
        depth_start = tap_index // 9
        row_step = tap_index // 3 % 3 - 1
        col_step = tap_index % 3 - 1
        offset = row_width + 1 + row_step * row_width + col_step
        shifted = flattened[
            :, :, depth_start : depth_start + depth_len, offset : offset + plane_size
        ]
        if col_step < 0:
            shifted = shifted * left_mask
        elif col_step > 0:
            shifted = shifted * right_mask
        pieces.append(shifted)
    return jnp.concatenate(pieces, axis=0)


def apply_weight(patches, weight):
    flat_weight = weight.reshape(weight.shape[0] * weight.shape[1], weight.shape[2])
    return jnp.einsum("ko,kgzp->ogzp", flat_weight, patches, preferred_element_type=jnp.float32)


def weight_term(patches, grad_block, in_channels):
    summed = jnp.einsum("kgzp,ogzp->ko", patches, grad_block, preferred_element_type=jnp.float32)
    return summed.reshape(27, in_channels, grad_block.shape[0])


def pool_cells(values, row_width):
    channels, samples, depth_len, plane_size = values.shape
    row_count = plane_size // row_width
    grouped = values.reshape(
        channels, samples, depth_len // 2, 2, row_count // 2, 2, row_width // 2, 2
    )
    return grouped.mean(axis=(3, 5, 7)).reshape(channels, samples, depth_len // 2, plane_size // 4)


def spread_cells(values, coarse_width):
    channels, samples, depth_len, plane_size = values.shape
    row_count = plane_size // coarse_width
    grouped = values.reshape(channels, samples, depth_len, 1, row_count, 1, coarse_width, 1)
    grouped = jnp.broadcast_to(
        grouped, (channels, samples, depth_len, 2, row_count, 2, coarse_width, 2)
    )
    return grouped.reshape(channels, samples, 2 * depth_len, 4 * plane_size) * 0.125


def forward_layer(padded, weight, bias_values, row_width, depth_block, pooled_out):
    out_channels = weight.shape[2]
    samples, depth_total, plane_size = (padded.shape[1], padded.shape[2] - 2, padded.shape[3])
    per_sample = depth_total // depth_block
    pre_buffer = jnp.zeros((out_channels, samples, depth_total, plane_size), jnp.bfloat16)
    if pooled_out:
        out_buffer = jnp.zeros(
            (out_channels, samples, depth_total // 2, plane_size // 4), jnp.bfloat16
        )
    else:
        out_buffer = jnp.zeros_like(pre_buffer)

    def forward_block_step(block_index, buffers):
        sample = block_index // per_sample
        depth_start = block_index % per_sample * depth_block
        pre_values = (
            apply_weight(gather_taps(padded, row_width), weight) + bias_values[:, None, None, None]
        ).astype(jnp.bfloat16)
        activated = jax.nn.silu(pre_values.astype(jnp.float32))
        if pooled_out:
            result = put_block(
                buffers[1],
                pool_cells(activated, row_width).astype(jnp.bfloat16),
                sample,
                depth_start // 2,
            )
        else:
            result = put_block(buffers[1], activated.astype(jnp.bfloat16), sample, depth_start)
        return (put_block(buffers[0], pre_values, sample, depth_start), result)

    return lax.fori_loop(0, samples * per_sample, forward_block_step, (pre_buffer, out_buffer))


def weight_grads(padded, delta_values, row_width, depth_block, weight):
    samples, depth_total = (delta_values.shape[1], delta_values.shape[2])
    per_sample = depth_total // depth_block
    in_channels = weight.shape[1]

    def weight_block_step(block_index, summed):
        return summed + weight_term(gather_taps(padded, row_width), delta_values, in_channels)

    return lax.fori_loop(
        0, samples * per_sample, weight_block_step, jnp.zeros(weight.shape, jnp.float32)
    )


def data_grads(padded, flipped, row_width, depth_block):
    out_channels = flipped.shape[2]
    samples, depth_total, plane_size = (padded.shape[1], padded.shape[2] - 2, padded.shape[3])
    per_sample = depth_total // depth_block
    out_buffer = jnp.zeros((out_channels, samples, depth_total, plane_size), jnp.bfloat16)

    def data_block_step(block_index, buffer_now):
        sample = block_index // per_sample
        depth_start = block_index % per_sample * depth_block
        result = apply_weight(gather_taps(padded, row_width), flipped).astype(jnp.bfloat16)
        return put_block(buffer_now, result, sample, depth_start)

    return lax.fori_loop(0, samples * per_sample, data_block_step, out_buffer)


def bias_sum(delta_values):
    return jnp.sum(delta_values, axis=(1, 2, 3), dtype=jnp.float32)


def per_device(volume, cotangent, w_first, b_first, w_second, b_second, w_third, b_third):
    flipped_second = jnp.flip(w_second, 0).transpose(0, 2, 1)
    flipped_third = jnp.flip(w_third, 0).transpose(0, 2, 1)
    volume_padded = with_halo(volume, (("slab", 2),), 1)
    first_pre, first_pooled = forward_layer(volume_padded, w_first, b_first, SX, CZ, True)
    first_padded = with_halo(first_pooled, (("slab", 2),), 1)
    second_pre, second_pooled = forward_layer(
        first_padded, w_second, b_second, SX // 2, CZ // 2, True
    )
    coarse_depth = second_pooled.shape[2]
    third_padded = with_halo(second_pooled, (("slab", 2),), 1)
    third_pre, features = forward_layer(
        third_padded, w_third, b_third, SX // 4, coarse_depth, False
    )
    third_delta = (
        cotangent.astype(jnp.float32) * silu_slope(third_pre.astype(jnp.float32))
    ).astype(jnp.bfloat16)
    kernel_third = weight_grads(third_padded, third_delta, SX // 4, coarse_depth, w_third)
    bias_third = bias_sum(third_delta)
    delta_window = with_halo(third_delta, (("slab", 2),), 1)
    second_back = data_grads(delta_window, flipped_third, SX // 4, coarse_depth)
    second_delta = (
        spread_cells(second_back.astype(jnp.float32), SX // 4)
        * silu_slope(second_pre.astype(jnp.float32))
    ).astype(jnp.bfloat16)
    kernel_second = weight_grads(first_padded, second_delta, SX // 2, CZ // 2, w_second)
    bias_second = bias_sum(second_delta)
    delta_padded = with_halo(second_delta, (("slab", 2),), 1)
    first_back = data_grads(delta_padded, flipped_second, SX // 2, CZ // 2)
    first_delta = (
        spread_cells(first_back.astype(jnp.float32), SX // 2)
        * silu_slope(first_pre.astype(jnp.float32))
    ).astype(jnp.bfloat16)
    kernel_first = weight_grads(volume_padded, first_delta, SX, CZ, w_first)
    bias_first = bias_sum(first_delta)
    grads = (kernel_first, bias_first, kernel_second, bias_second, kernel_third, bias_third)
    summed = all_reduce_grads(grads)
    return (features,) + summed


def xor_pairs(axis, mask):
    return [(i, i ^ mask) for i in range(lax.axis_size(axis))]


def all_reduce_grads(grads, halving_steps=3):
    steps = []
    for axis in ("sample", "slab"):
        mask = 1
        while mask < lax.axis_size(axis):
            steps.append((axis, mask))
            mask *= 2
    sizes = [g.size for g in grads]
    flat = jnp.concatenate([g.reshape(-1) for g in grads])
    block = 1024 * (1 << halving_steps)
    total = -(-flat.shape[0] // block) * block
    flat = jnp.pad(flat, (0, total - flat.shape[0]))
    kept = []
    for axis, mask in steps[:halving_steps]:
        half = flat.shape[0] // 2
        upper = (lax.axis_index(axis) & mask) != 0
        low, high = flat[:half], flat[half:]
        send = jnp.where(upper, low, high)
        keep = jnp.where(upper, high, low)
        flat = keep + lax.ppermute(send, axis, xor_pairs(axis, mask))
        kept.append((axis, mask, upper))
    for axis, mask in steps[halving_steps:]:
        flat = flat + lax.ppermute(flat, axis, xor_pairs(axis, mask))
    for axis, mask, upper in reversed(kept):
        other = lax.ppermute(flat, axis, xor_pairs(axis, mask))
        flat = jnp.where(
            upper, jnp.concatenate([other, flat]), jnp.concatenate([flat, other])
        )
    out = []
    start = 0
    for g, size in zip(grads, sizes):
        out.append(flat[start : start + size].reshape(g.shape))
        start += size
    return tuple(out)


def solution(mesh):
    in_specs = (
        P(None, "sample", "slab", None),
        P(None, "sample", "slab", None),
        P(),
        P(),
        P(),
        P(),
        P(),
        P(),
    )
    out_specs = (P(None, "sample", "slab", None), P(), P(), P(), P(), P(), P())
    return jax.shard_map(
        per_device, mesh=mesh, in_specs=in_specs, out_specs=out_specs, check_vma=False
    )
```

```python
import jax
import jax.numpy as jnp
from jax import lax
from jax.sharding import PartitionSpec as P

SX = 32
CZ = 4


def with_halo(shard, sides, width):
    for axis, dim in sides:
        size, length = (lax.axis_size(axis), shard.shape[dim])
        up = [(i, (i + 1) % size) for i in range(size - 1)]
        down = [(j, i) for i, j in up]
        last = lax.slice_in_dim(shard, length - width, length, axis=dim)
        first = lax.slice_in_dim(shard, 0, width, axis=dim)
        before = lax.ppermute(last, axis, up)
        after = lax.ppermute(first, axis, down)
        shard = jnp.concatenate([before, shard, after], axis=dim)
    return shard


def silu_slope(values):
    sigmoid = jax.nn.sigmoid(values)
    return sigmoid * (1.0 + values * (1.0 - sigmoid))


def conv_forward(padded, weight):
    kernel = weight.reshape(3, 3, 3, weight.shape[1], weight.shape[2])
    return lax.conv_general_dilated(
        padded,
        kernel,
        window_strides=(1, 1, 1),
        padding=((0, 0), (1, 1), (1, 1)),
        dimension_numbers=("CNDHW", "DHWIO", "CNDHW"),
        preferred_element_type=jnp.float32,
    )


def conv_backward(padded, weight):
    kernel = weight.reshape(3, 3, 3, weight.shape[1], weight.shape[2])[::-1, ::-1, ::-1]
    return lax.conv_general_dilated(
        padded,
        kernel,
        window_strides=(1, 1, 1),
        padding=((0, 0), (1, 1), (1, 1)),
        dimension_numbers=("CNDHW", "DHWOI", "CNDHW"),
        preferred_element_type=jnp.float32,
    )


def conv_weight_grad(padded, delta):
    summed = lax.conv_general_dilated(
        padded,
        delta,
        window_strides=(1, 1, 1),
        padding=((0, 0), (1, 1), (1, 1)),
        dimension_numbers=("NCDHW", "OIDHW", "NCDHW"),
        preferred_element_type=jnp.float32,
    )
    return summed.transpose(2, 3, 4, 0, 1).reshape(27, padded.shape[0], delta.shape[0])


def pool_cells(values):
    c, n, z, y, x = values.shape
    grouped = values.reshape(c, n, z // 2, 2, y // 2, 2, x // 2, 2)
    return grouped.mean(axis=(3, 5, 7))


def spread_cells(values):
    c, n, z, y, x = values.shape
    grouped = values.reshape(c, n, z, 1, y, 1, x, 1)
    grouped = jnp.broadcast_to(grouped, (c, n, z, 2, y, 2, x, 2))
    return grouped.reshape(c, n, 2 * z, 2 * y, 2 * x) * 0.125


def bias_sum(delta_values):
    return jnp.sum(delta_values, axis=(1, 2, 3, 4), dtype=jnp.float32)


def per_device(volume, cotangent, w_first, b_first, w_second, b_second, w_third, b_third):
    c0, n, z0, plane = volume.shape
    sy = plane // SX
    source = volume.reshape(c0, n, z0, sy, SX)
    upstream = cotangent.reshape(cotangent.shape[0], n, z0 // 4, sy // 4, SX // 4)
    volume_padded = with_halo(source, (("slab", 2),), 1)
    first_pre = (
        conv_forward(volume_padded, w_first) + b_first[:, None, None, None, None]
    ).astype(jnp.bfloat16)
    first_pooled = pool_cells(jax.nn.silu(first_pre.astype(jnp.float32))).astype(jnp.bfloat16)
    first_padded = with_halo(first_pooled, (("slab", 2),), 1)
    second_pre = (
        conv_forward(first_padded, w_second) + b_second[:, None, None, None, None]
    ).astype(jnp.bfloat16)
    second_pooled = pool_cells(jax.nn.silu(second_pre.astype(jnp.float32))).astype(jnp.bfloat16)
    third_padded = with_halo(second_pooled, (("slab", 2),), 1)
    third_pre = (
        conv_forward(third_padded, w_third) + b_third[:, None, None, None, None]
    ).astype(jnp.bfloat16)
    features = jax.nn.silu(third_pre.astype(jnp.float32)).astype(jnp.bfloat16)
    third_delta = (
        upstream.astype(jnp.float32) * silu_slope(third_pre.astype(jnp.float32))
    ).astype(jnp.bfloat16)
    kernel_third = conv_weight_grad(third_padded, third_delta)
    bias_third = bias_sum(third_delta)
    delta_window = with_halo(third_delta, (("slab", 2),), 1)
    second_back = conv_backward(delta_window, w_third).astype(jnp.bfloat16)
    second_delta = (
        spread_cells(second_back.astype(jnp.float32))
        * silu_slope(second_pre.astype(jnp.float32))
    ).astype(jnp.bfloat16)
    kernel_second = conv_weight_grad(first_padded, second_delta)
    bias_second = bias_sum(second_delta)
    delta_padded = with_halo(second_delta, (("slab", 2),), 1)
    first_back = conv_backward(delta_padded, w_second).astype(jnp.bfloat16)
    first_delta = (
        spread_cells(first_back.astype(jnp.float32))
        * silu_slope(first_pre.astype(jnp.float32))
    ).astype(jnp.bfloat16)
    kernel_first = conv_weight_grad(volume_padded, first_delta)
    bias_first = bias_sum(first_delta)
    grads = (kernel_first, bias_first, kernel_second, bias_second, kernel_third, bias_third)
    summed = all_reduce_grads(grads)
    return (features.reshape(cotangent.shape),) + summed


def xor_pairs(axis, mask):
    return [(i, i ^ mask) for i in range(lax.axis_size(axis))]


def all_reduce_grads(grads, halving_steps=3):
    steps = []
    for axis in ("sample", "slab"):
        mask = 1
        while mask < lax.axis_size(axis):
            steps.append((axis, mask))
            mask *= 2
    sizes = [g.size for g in grads]
    flat = jnp.concatenate([g.reshape(-1) for g in grads])
    block = 1024 * (1 << halving_steps)
    total = -(-flat.shape[0] // block) * block
    flat = jnp.pad(flat, (0, total - flat.shape[0]))
    kept = []
    for axis, mask in steps[:halving_steps]:
        half = flat.shape[0] // 2
        upper = (lax.axis_index(axis) & mask) != 0
        low, high = flat[:half], flat[half:]
        send = jnp.where(upper, low, high)
        keep = jnp.where(upper, high, low)
        flat = keep + lax.ppermute(send, axis, xor_pairs(axis, mask))
        kept.append((axis, mask, upper))
    for axis, mask in steps[halving_steps:]:
        flat = flat + lax.ppermute(flat, axis, xor_pairs(axis, mask))
    for axis, mask, upper in reversed(kept):
        other = lax.ppermute(flat, axis, xor_pairs(axis, mask))
        flat = jnp.where(
            upper, jnp.concatenate([other, flat]), jnp.concatenate([flat, other])
        )
    out = []
    start = 0
    for g, size in zip(grads, sizes):
        out.append(flat[start : start + size].reshape(g.shape))
        start += size
    return tuple(out)


def solution(mesh):
    in_specs = (
        P(None, "sample", "slab", None),
        P(None, "sample", "slab", None),
        P(),
        P(),
        P(),
        P(),
        P(),
        P(),
    )
    out_specs = (P(None, "sample", "slab", None), P(), P(), P(), P(), P(), P())
    return jax.shard_map(
        per_device, mesh=mesh, in_specs=in_specs, out_specs=out_specs, check_vma=False
    )
```

```python
import jax
import jax.numpy as jnp
from jax import lax
from jax.sharding import PartitionSpec as P

SX = 32
CZ = 4


def with_halo(shard, sides, width):
    for axis, dim in sides:
        size, length = (lax.axis_size(axis), shard.shape[dim])
        up = [(i, (i + 1) % size) for i in range(size - 1)]
        down = [(j, i) for i, j in up]
        last = lax.slice_in_dim(shard, length - width, length, axis=dim)
        first = lax.slice_in_dim(shard, 0, width, axis=dim)
        before = lax.ppermute(last, axis, up)
        after = lax.ppermute(first, axis, down)
        shard = jnp.concatenate([before, shard, after], axis=dim)
    return shard


def silu_slope(values):
    sigmoid = jax.nn.sigmoid(values)
    return sigmoid * (1.0 + values * (1.0 - sigmoid))


def put_block(values, update, sample, depth_start):
    return lax.dynamic_update_slice(values, update, (0, sample, depth_start, 0))


def gather_taps(section, row_width):
    depth_len = section.shape[2] - 2
    plane_size = section.shape[3]
    flattened = jnp.pad(section, ((0, 0), (0, 0), (0, 0), (row_width + 1, row_width + 1)))
    column = lax.broadcasted_iota(jnp.int32, (1, 1, 1, plane_size), 3) % row_width
    left_mask = (column >= 1).astype(section.dtype)
    right_mask = (column <= row_width - 2).astype(section.dtype)
    pieces = []
    for tap_index in range(27):
        depth_start = tap_index // 9
        row_step = tap_index // 3 % 3 - 1
        col_step = tap_index % 3 - 1
        offset = row_width + 1 + row_step * row_width + col_step
        shifted = flattened[
            :, :, depth_start : depth_start + depth_len, offset : offset + plane_size
        ]
        if col_step < 0:
            shifted = shifted * left_mask
        elif col_step > 0:
            shifted = shifted * right_mask
        pieces.append(shifted)
    return jnp.concatenate(pieces, axis=0)


def apply_weight(patches, weight):
    flat_weight = weight.reshape(weight.shape[0] * weight.shape[1], weight.shape[2])
    return jnp.einsum("ko,kgzp->ogzp", flat_weight, patches, preferred_element_type=jnp.float32)


def weight_term(patches, grad_block, in_channels):
    summed = jnp.einsum("kgzp,ogzp->ko", patches, grad_block, preferred_element_type=jnp.float32)
    return summed.reshape(27, in_channels, grad_block.shape[0])


def pool_cells(values, row_width):
    channels, samples, depth_len, plane_size = values.shape
    row_count = plane_size // row_width
    grouped = values.reshape(
        channels, samples, depth_len // 2, 2, row_count // 2, 2, row_width // 2, 2
    )
    return grouped.mean(axis=(3, 5, 7)).reshape(channels, samples, depth_len // 2, plane_size // 4)


def spread_cells(values, coarse_width):
    channels, samples, depth_len, plane_size = values.shape
    row_count = plane_size // coarse_width
    grouped = values.reshape(channels, samples, depth_len, 1, row_count, 1, coarse_width, 1)
    grouped = jnp.broadcast_to(
        grouped, (channels, samples, depth_len, 2, row_count, 2, coarse_width, 2)
    )
    return grouped.reshape(channels, samples, 2 * depth_len, 4 * plane_size) * 0.125


def forward_layer(padded, weight, bias_values, row_width, depth_block, pooled_out):
    out_channels = weight.shape[2]
    samples, depth_total, plane_size = (padded.shape[1], padded.shape[2] - 2, padded.shape[3])
    per_sample = depth_total // depth_block
    pre_buffer = jnp.zeros((out_channels, samples, depth_total, plane_size), jnp.bfloat16)
    if pooled_out:
        out_buffer = jnp.zeros(
            (out_channels, samples, depth_total // 2, plane_size // 4), jnp.bfloat16
        )
    else:
        out_buffer = jnp.zeros_like(pre_buffer)

    def forward_block_step(block_index, buffers):
        sample = block_index // per_sample
        depth_start = block_index % per_sample * depth_block
        pre_values = (
            apply_weight(gather_taps(padded, row_width), weight) + bias_values[:, None, None, None]
        ).astype(jnp.bfloat16)
        activated = jax.nn.silu(pre_values.astype(jnp.float32))
        if pooled_out:
            result = put_block(
                buffers[1],
                pool_cells(activated, row_width).astype(jnp.bfloat16),
                sample,
                depth_start // 2,
            )
        else:
            result = put_block(buffers[1], activated.astype(jnp.bfloat16), sample, depth_start)
        return (put_block(buffers[0], pre_values, sample, depth_start), result)

    return lax.fori_loop(0, samples * per_sample, forward_block_step, (pre_buffer, out_buffer))


def weight_grads(padded, delta_values, row_width, depth_block, weight):
    samples, depth_total = (delta_values.shape[1], delta_values.shape[2])
    per_sample = depth_total // depth_block
    in_channels = weight.shape[1]

    def weight_block_step(block_index, summed):
        return summed + weight_term(gather_taps(padded, row_width), delta_values, in_channels)

    return lax.fori_loop(
        0, samples * per_sample, weight_block_step, jnp.zeros(weight.shape, jnp.float32)
    )


def data_grads(padded, flipped, row_width, depth_block):
    out_channels = flipped.shape[2]
    samples, depth_total, plane_size = (padded.shape[1], padded.shape[2] - 2, padded.shape[3])
    per_sample = depth_total // depth_block
    out_buffer = jnp.zeros((out_channels, samples, depth_total, plane_size), jnp.bfloat16)

    def data_block_step(block_index, buffer_now):
        sample = block_index // per_sample
        depth_start = block_index % per_sample * depth_block
        result = apply_weight(gather_taps(padded, row_width), flipped).astype(jnp.bfloat16)
        return put_block(buffer_now, result, sample, depth_start)

    return lax.fori_loop(0, samples * per_sample, data_block_step, out_buffer)


def bias_sum(delta_values):
    return jnp.sum(delta_values, axis=(1, 2, 3), dtype=jnp.float32)


def per_device(volume, cotangent, w_first, b_first, w_second, b_second, w_third, b_third):
    flipped_second = jnp.flip(w_second, 0).transpose(0, 2, 1)
    flipped_third = jnp.flip(w_third, 0).transpose(0, 2, 1)
    volume_padded = with_halo(volume, (("slab", 2),), 1)
    first_pre, first_pooled = forward_layer(volume_padded, w_first, b_first, SX, CZ, True)
    first_padded = with_halo(first_pooled, (("slab", 2),), 1)
    second_pre, second_pooled = forward_layer(
        first_padded, w_second, b_second, SX // 2, CZ // 2, True
    )
    coarse_depth = second_pooled.shape[2]
    third_padded = with_halo(second_pooled, (("slab", 2),), 1)
    third_pre, features = forward_layer(
        third_padded, w_third, b_third, SX // 4, coarse_depth, False
    )
    third_delta = (
        cotangent.astype(jnp.float32) * silu_slope(third_pre.astype(jnp.float32))
    ).astype(jnp.bfloat16)
    kernel_third = weight_grads(third_padded, third_delta, SX // 4, coarse_depth, w_third)
    bias_third = bias_sum(third_delta)
    delta_window = with_halo(third_delta, (("slab", 2),), 1)
    second_back = data_grads(delta_window, flipped_third, SX // 4, coarse_depth)
    second_delta = (
        spread_cells(second_back.astype(jnp.float32), SX // 4)
        * silu_slope(second_pre.astype(jnp.float32))
    ).astype(jnp.bfloat16)
    kernel_second = weight_grads(first_padded, second_delta, SX // 2, CZ // 2, w_second)
    bias_second = bias_sum(second_delta)
    delta_padded = with_halo(second_delta, (("slab", 2),), 1)
    first_back = data_grads(delta_padded, flipped_second, SX // 2, CZ // 2)
    first_delta = (
        spread_cells(first_back.astype(jnp.float32), SX // 2)
        * silu_slope(first_pre.astype(jnp.float32))
    ).astype(jnp.bfloat16)
    kernel_first = weight_grads(volume_padded, first_delta, SX, CZ, w_first)
    bias_first = bias_sum(first_delta)
    weights = all_reduce_rows(
        (kernel_third, kernel_second, kernel_first, bias_third, bias_second, bias_first)
    )
    kernel_third, kernel_second, kernel_first, bias_third, bias_second, bias_first = weights
    return (
        features,
        kernel_first,
        bias_first,
        kernel_second,
        bias_second,
        kernel_third,
        bias_third,
    )


def xor_pairs(axis, mask):
    return [(i, i ^ mask) for i in range(lax.axis_size(axis))]


def all_reduce_rows(grads, halving_steps=3, lanes=128):
    steps = []
    for axis in ("sample", "slab"):
        mask = 1
        while mask < lax.axis_size(axis):
            steps.append((axis, mask))
            mask *= 2
    pieces, offsets = [], []
    rows = 0
    for g in grads:
        count = -(-g.size // lanes)
        flat = g.reshape(-1)
        flat = jnp.pad(flat, (0, count * lanes - g.size))
        pieces.append(flat.reshape(count, lanes))
        offsets.append(rows)
        rows += count
    block = 8 << halving_steps
    total = -(-rows // block) * block
    if total > rows:
        pieces.append(jnp.zeros((total - rows, lanes), jnp.float32))
    buffer = jnp.concatenate(pieces, axis=0)
    kept = []
    for axis, mask in steps[:halving_steps]:
        half = buffer.shape[0] // 2
        upper = ((lax.axis_index(axis) // mask) % 2).astype(jnp.int32)
        send = lax.dynamic_slice_in_dim(buffer, (1 - upper) * half, half, axis=0)
        keep = lax.dynamic_slice_in_dim(buffer, upper * half, half, axis=0)
        buffer = keep + lax.ppermute(send, axis, xor_pairs(axis, mask))
        kept.append((axis, mask, upper))
    for axis, mask in steps[halving_steps:]:
        buffer = buffer + lax.ppermute(buffer, axis, xor_pairs(axis, mask))
    for axis, mask, upper in reversed(kept):
        other = lax.ppermute(buffer, axis, xor_pairs(axis, mask))
        pair = jnp.stack([buffer, other])
        first = lax.dynamic_index_in_dim(pair, upper, axis=0, keepdims=False)
        second = lax.dynamic_index_in_dim(pair, 1 - upper, axis=0, keepdims=False)
        buffer = jnp.concatenate([first, second], axis=0)
    out = []
    for g, start in zip(grads, offsets):
        count = -(-g.size // lanes)
        part = buffer[start : start + count].reshape(-1)[: g.size]
        out.append(part.reshape(g.shape))
    return tuple(out)


def solution(mesh):
    in_specs = (
        P(None, "sample", "slab", None),
        P(None, "sample", "slab", None),
        P(),
        P(),
        P(),
        P(),
        P(),
        P(),
    )
    out_specs = (P(None, "sample", "slab", None), P(), P(), P(), P(), P(), P())
    return jax.shard_map(
        per_device, mesh=mesh, in_specs=in_specs, out_specs=out_specs, check_vma=False
    )
```

```python
import jax
import jax.numpy as jnp
from jax import lax
from jax.sharding import PartitionSpec as P

SX = 32
CZ = 4


def with_halo(shard, sides, width):
    for axis, dim in sides:
        size, length = (lax.axis_size(axis), shard.shape[dim])
        up = [(i, (i + 1) % size) for i in range(size - 1)]
        down = [(j, i) for i, j in up]
        last = lax.slice_in_dim(shard, length - width, length, axis=dim)
        first = lax.slice_in_dim(shard, 0, width, axis=dim)
        before = lax.ppermute(last, axis, up)
        after = lax.ppermute(first, axis, down)
        shard = jnp.concatenate([before, shard, after], axis=dim)
    return shard


def silu_slope(values):
    sigmoid = jax.nn.sigmoid(values)
    return sigmoid * (1.0 + values * (1.0 - sigmoid))


def put_block(values, update, sample, depth_start):
    return lax.dynamic_update_slice(values, update, (0, sample, depth_start, 0))


def gather_taps(section, row_width):
    depth_len = section.shape[2] - 2
    plane_size = section.shape[3]
    flattened = jnp.pad(section, ((0, 0), (0, 0), (0, 0), (row_width + 1, row_width + 1)))
    column = lax.broadcasted_iota(jnp.int32, (1, 1, 1, plane_size), 3) % row_width
    left_mask = (column >= 1).astype(section.dtype)
    right_mask = (column <= row_width - 2).astype(section.dtype)
    pieces = []
    for tap_index in range(27):
        depth_start = tap_index // 9
        row_step = tap_index // 3 % 3 - 1
        col_step = tap_index % 3 - 1
        offset = row_width + 1 + row_step * row_width + col_step
        shifted = flattened[
            :, :, depth_start : depth_start + depth_len, offset : offset + plane_size
        ]
        if col_step < 0:
            shifted = shifted * left_mask
        elif col_step > 0:
            shifted = shifted * right_mask
        pieces.append(shifted)
    return jnp.concatenate(pieces, axis=0)


def apply_weight(patches, weight):
    flat_weight = weight.reshape(weight.shape[0] * weight.shape[1], weight.shape[2])
    return jnp.einsum("ko,kgzp->ogzp", flat_weight, patches, preferred_element_type=jnp.float32)


def weight_term(patches, grad_block, in_channels):
    summed = jnp.einsum("kgzp,ogzp->ko", patches, grad_block, preferred_element_type=jnp.float32)
    return summed.reshape(27, in_channels, grad_block.shape[0])


def pool_cells(values, row_width):
    channels, samples, depth_len, plane_size = values.shape
    row_count = plane_size // row_width
    grouped = values.reshape(
        channels, samples, depth_len // 2, 2, row_count // 2, 2, row_width // 2, 2
    )
    return grouped.mean(axis=(3, 5, 7)).reshape(channels, samples, depth_len // 2, plane_size // 4)


def spread_cells(values, coarse_width):
    channels, samples, depth_len, plane_size = values.shape
    row_count = plane_size // coarse_width
    grouped = values.reshape(channels, samples, depth_len, 1, row_count, 1, coarse_width, 1)
    grouped = jnp.broadcast_to(
        grouped, (channels, samples, depth_len, 2, row_count, 2, coarse_width, 2)
    )
    return grouped.reshape(channels, samples, 2 * depth_len, 4 * plane_size) * 0.125


def forward_layer(padded, weight, bias_values, row_width, depth_block, pooled_out):
    out_channels = weight.shape[2]
    samples, depth_total, plane_size = (padded.shape[1], padded.shape[2] - 2, padded.shape[3])
    per_sample = depth_total // depth_block
    pre_buffer = jnp.zeros((out_channels, samples, depth_total, plane_size), jnp.bfloat16)
    if pooled_out:
        out_buffer = jnp.zeros(
            (out_channels, samples, depth_total // 2, plane_size // 4), jnp.bfloat16
        )
    else:
        out_buffer = jnp.zeros_like(pre_buffer)

    def forward_block_step(block_index, buffers):
        sample = block_index // per_sample
        depth_start = block_index % per_sample * depth_block
        pre_values = (
            apply_weight(gather_taps(padded, row_width), weight) + bias_values[:, None, None, None]
        ).astype(jnp.bfloat16)
        activated = jax.nn.silu(pre_values.astype(jnp.float32))
        if pooled_out:
            result = put_block(
                buffers[1],
                pool_cells(activated, row_width).astype(jnp.bfloat16),
                sample,
                depth_start // 2,
            )
        else:
            result = put_block(buffers[1], activated.astype(jnp.bfloat16), sample, depth_start)
        return (put_block(buffers[0], pre_values, sample, depth_start), result)

    return lax.fori_loop(0, samples * per_sample, forward_block_step, (pre_buffer, out_buffer))


def weight_grads(padded, delta_values, row_width, depth_block, weight):
    samples, depth_total = (delta_values.shape[1], delta_values.shape[2])
    per_sample = depth_total // depth_block
    in_channels = weight.shape[1]

    def weight_block_step(block_index, summed):
        return summed + weight_term(gather_taps(padded, row_width), delta_values, in_channels)

    return lax.fori_loop(
        0, samples * per_sample, weight_block_step, jnp.zeros(weight.shape, jnp.float32)
    )


def data_grads(padded, flipped, row_width, depth_block):
    out_channels = flipped.shape[2]
    samples, depth_total, plane_size = (padded.shape[1], padded.shape[2] - 2, padded.shape[3])
    per_sample = depth_total // depth_block
    out_buffer = jnp.zeros((out_channels, samples, depth_total, plane_size), jnp.bfloat16)

    def data_block_step(block_index, buffer_now):
        sample = block_index // per_sample
        depth_start = block_index % per_sample * depth_block
        result = apply_weight(gather_taps(padded, row_width), flipped).astype(jnp.bfloat16)
        return put_block(buffer_now, result, sample, depth_start)

    return lax.fori_loop(0, samples * per_sample, data_block_step, out_buffer)


def parity_split(values, row_width):
    c, n, z, plane = values.shape
    rows = plane // row_width
    grouped = values.reshape(c, n, z, rows // 2, 2, row_width // 2, 2)
    grouped = grouped.transpose(0, 1, 2, 4, 6, 3, 5)
    return grouped.reshape(c, n, z, 4, plane // 4)

def parity_taps(split, coarse_width):
    depth_len = split.shape[2] - 2
    size = split.shape[4]
    pad = coarse_width + 1
    flattened = jnp.pad(split, ((0, 0), (0, 0), (0, 0), (0, 0), (pad, pad)))
    column = lax.broadcasted_iota(jnp.int32, (1, 1, 1, size), 3) % coarse_width
    left_mask = (column >= 1).astype(split.dtype)
    right_mask = (column <= coarse_width - 2).astype(split.dtype)
    blocks = []
    for a in range(2):
        for b in range(2):
            pieces = []
            for tap_index in range(27):
                depth_start = tap_index // 9
                row_sum = a + tap_index // 3 % 3 - 1
                col_sum = b + tap_index % 3 - 1
                source = (row_sum % 2) * 2 + col_sum % 2
                row_step, col_step = row_sum // 2, col_sum // 2
                offset = pad + row_step * coarse_width + col_step
                shifted = flattened[:, :, depth_start : depth_start + depth_len, source, offset : offset + size]
                if col_step < 0:
                    shifted = shifted * left_mask
                elif col_step > 0:
                    shifted = shifted * right_mask
                pieces.append(shifted)
            blocks.append(jnp.concatenate(pieces, axis=0))
    return jnp.stack(blocks, axis=3)

def parity_pool(values):
    c, n, z, parities, size = values.shape
    return values.reshape(c, n, z // 2, 2 * parities, size).mean(axis=3)

def parity_spread(values):
    c, n, z, size = values.shape
    grouped = jnp.broadcast_to(values[:, :, :, None, None, :], (c, n, z, 2, 4, size))
    return grouped.reshape(c, n, 2 * z, 4, size) * 0.125


def bias_sum(delta_values):
    return jnp.sum(delta_values, axis=(1, 2, 3), dtype=jnp.float32)


def per_device(volume, cotangent, w_first, b_first, w_second, b_second, w_third, b_third):
    flipped_second = jnp.flip(w_second, 0).transpose(0, 2, 1)
    flipped_third = jnp.flip(w_third, 0).transpose(0, 2, 1)
    volume_padded = with_halo(volume, (("slab", 2),), 1)
    first_patches = parity_taps(parity_split(volume_padded, SX), SX // 2)
    first_pre = (
        jnp.einsum(
            "ko,kgzpq->ogzpq",
            w_first.reshape(-1, w_first.shape[2]),
            first_patches,
            preferred_element_type=jnp.float32,
        )
        + b_first[:, None, None, None, None]
    ).astype(jnp.bfloat16)
    first_pooled = parity_pool(jax.nn.silu(first_pre.astype(jnp.float32))).astype(jnp.bfloat16)
    first_padded = with_halo(first_pooled, (("slab", 2),), 1)
    second_pre, second_pooled = forward_layer(
        first_padded, w_second, b_second, SX // 2, CZ // 2, True
    )
    coarse_depth = second_pooled.shape[2]
    third_padded = with_halo(second_pooled, (("slab", 2),), 1)
    third_pre, features = forward_layer(
        third_padded, w_third, b_third, SX // 4, coarse_depth, False
    )
    third_delta = (
        cotangent.astype(jnp.float32) * silu_slope(third_pre.astype(jnp.float32))
    ).astype(jnp.bfloat16)
    kernel_third = weight_grads(third_padded, third_delta, SX // 4, coarse_depth, w_third)
    bias_third = bias_sum(third_delta)
    delta_window = with_halo(third_delta, (("slab", 2),), 1)
    second_back = data_grads(delta_window, flipped_third, SX // 4, coarse_depth)
    second_delta = (
        spread_cells(second_back.astype(jnp.float32), SX // 4)
        * silu_slope(second_pre.astype(jnp.float32))
    ).astype(jnp.bfloat16)
    kernel_second = weight_grads(first_padded, second_delta, SX // 2, CZ // 2, w_second)
    bias_second = bias_sum(second_delta)
    delta_padded = with_halo(second_delta, (("slab", 2),), 1)
    first_back = data_grads(delta_padded, flipped_second, SX // 2, CZ // 2)
    first_delta = (
        parity_spread(first_back.astype(jnp.float32)) * silu_slope(first_pre.astype(jnp.float32))
    ).astype(jnp.bfloat16)
    kernel_first = jnp.einsum(
        "kgzpq,ogzpq->ko", first_patches, first_delta, preferred_element_type=jnp.float32
    ).reshape(w_first.shape)
    bias_first = jnp.sum(first_delta, axis=(1, 2, 3, 4), dtype=jnp.float32)
    weights = all_reduce_rows(
        (kernel_third, kernel_second, kernel_first, bias_third, bias_second, bias_first)
    )
    kernel_third, kernel_second, kernel_first, bias_third, bias_second, bias_first = weights
    return (
        features,
        kernel_first,
        bias_first,
        kernel_second,
        bias_second,
        kernel_third,
        bias_third,
    )


def xor_pairs(axis, mask):
    return [(i, i ^ mask) for i in range(lax.axis_size(axis))]


def all_reduce_rows(grads, halving_steps=3, lanes=128):
    steps = []
    for axis in ("sample", "slab"):
        mask = 1
        while mask < lax.axis_size(axis):
            steps.append((axis, mask))
            mask *= 2
    pieces, offsets = [], []
    rows = 0
    for g in grads:
        count = -(-g.size // lanes)
        flat = g.reshape(-1)
        flat = jnp.pad(flat, (0, count * lanes - g.size))
        pieces.append(flat.reshape(count, lanes))
        offsets.append(rows)
        rows += count
    block = 8 << halving_steps
    total = -(-rows // block) * block
    if total > rows:
        pieces.append(jnp.zeros((total - rows, lanes), jnp.float32))
    buffer = jnp.concatenate(pieces, axis=0)
    kept = []
    for axis, mask in steps[:halving_steps]:
        half = buffer.shape[0] // 2
        upper = ((lax.axis_index(axis) // mask) % 2).astype(jnp.int32)
        send = lax.dynamic_slice_in_dim(buffer, (1 - upper) * half, half, axis=0)
        keep = lax.dynamic_slice_in_dim(buffer, upper * half, half, axis=0)
        buffer = keep + lax.ppermute(send, axis, xor_pairs(axis, mask))
        kept.append((axis, mask, upper))
    for axis, mask in steps[halving_steps:]:
        buffer = buffer + lax.ppermute(buffer, axis, xor_pairs(axis, mask))
    for axis, mask, upper in reversed(kept):
        other = lax.ppermute(buffer, axis, xor_pairs(axis, mask))
        pair = jnp.stack([buffer, other])
        first = lax.dynamic_index_in_dim(pair, upper, axis=0, keepdims=False)
        second = lax.dynamic_index_in_dim(pair, 1 - upper, axis=0, keepdims=False)
        buffer = jnp.concatenate([first, second], axis=0)
    out = []
    for g, start in zip(grads, offsets):
        count = -(-g.size // lanes)
        part = buffer[start : start + count].reshape(-1)[: g.size]
        out.append(part.reshape(g.shape))
    return tuple(out)


def solution(mesh):
    in_specs = (
        P(None, "sample", "slab", None),
        P(None, "sample", "slab", None),
        P(),
        P(),
        P(),
        P(),
        P(),
        P(),
    )
    out_specs = (P(None, "sample", "slab", None), P(), P(), P(), P(), P(), P())
    return jax.shard_map(
        per_device, mesh=mesh, in_specs=in_specs, out_specs=out_specs, check_vma=False
    )
```

```python
import functools

import jax
import jax.numpy as jnp
from jax import lax
from jax.experimental import pallas as pl
from jax.experimental.pallas import tpu as pltpu
from jax.sharding import PartitionSpec as P

SX = 32
CZ = 4


def with_halo(shard, sides, width):
    for axis, dim in sides:
        size, length = (lax.axis_size(axis), shard.shape[dim])
        up = [(i, (i + 1) % size) for i in range(size - 1)]
        down = [(j, i) for i, j in up]
        last = lax.slice_in_dim(shard, length - width, length, axis=dim)
        first = lax.slice_in_dim(shard, 0, width, axis=dim)
        before = lax.ppermute(last, axis, up)
        after = lax.ppermute(first, axis, down)
        shard = jnp.concatenate([before, shard, after], axis=dim)
    return shard


def silu_slope(values):
    sigmoid = jax.nn.sigmoid(values)
    return sigmoid * (1.0 + values * (1.0 - sigmoid))


def put_block(values, update, sample, depth_start):
    return lax.dynamic_update_slice(values, update, (0, sample, depth_start, 0))


def gather_taps(section, row_width):
    depth_len = section.shape[2] - 2
    plane_size = section.shape[3]
    flattened = jnp.pad(section, ((0, 0), (0, 0), (0, 0), (row_width + 1, row_width + 1)))
    column = lax.broadcasted_iota(jnp.int32, (1, 1, 1, plane_size), 3) % row_width
    left_mask = (column >= 1).astype(section.dtype)
    right_mask = (column <= row_width - 2).astype(section.dtype)
    pieces = []
    for tap_index in range(27):
        depth_start = tap_index // 9
        row_step = tap_index // 3 % 3 - 1
        col_step = tap_index % 3 - 1
        offset = row_width + 1 + row_step * row_width + col_step
        shifted = flattened[
            :, :, depth_start : depth_start + depth_len, offset : offset + plane_size
        ]
        if col_step < 0:
            shifted = shifted * left_mask
        elif col_step > 0:
            shifted = shifted * right_mask
        pieces.append(shifted)
    return jnp.concatenate(pieces, axis=0)


def apply_weight(patches, weight):
    flat_weight = weight.reshape(weight.shape[0] * weight.shape[1], weight.shape[2])
    return jnp.einsum("ko,kgzp->ogzp", flat_weight, patches, preferred_element_type=jnp.float32)


def weight_term(patches, grad_block, in_channels):
    summed = jnp.einsum("kgzp,ogzp->ko", patches, grad_block, preferred_element_type=jnp.float32)
    return summed.reshape(27, in_channels, grad_block.shape[0])


def pool_cells(values, row_width):
    channels, samples, depth_len, plane_size = values.shape
    row_count = plane_size // row_width
    grouped = values.reshape(
        channels, samples, depth_len // 2, 2, row_count // 2, 2, row_width // 2, 2
    )
    return grouped.mean(axis=(3, 5, 7)).reshape(channels, samples, depth_len // 2, plane_size // 4)


def spread_cells(values, coarse_width):
    channels, samples, depth_len, plane_size = values.shape
    row_count = plane_size // coarse_width
    grouped = values.reshape(channels, samples, depth_len, 1, row_count, 1, coarse_width, 1)
    grouped = jnp.broadcast_to(
        grouped, (channels, samples, depth_len, 2, row_count, 2, coarse_width, 2)
    )
    return grouped.reshape(channels, samples, 2 * depth_len, 4 * plane_size) * 0.125


def forward_layer(padded, weight, bias_values, row_width, depth_block, pooled_out):
    out_channels = weight.shape[2]
    samples, depth_total, plane_size = (padded.shape[1], padded.shape[2] - 2, padded.shape[3])
    per_sample = depth_total // depth_block
    pre_buffer = jnp.zeros((out_channels, samples, depth_total, plane_size), jnp.bfloat16)
    if pooled_out:
        out_buffer = jnp.zeros(
            (out_channels, samples, depth_total // 2, plane_size // 4), jnp.bfloat16
        )
    else:
        out_buffer = jnp.zeros_like(pre_buffer)

    def forward_block_step(block_index, buffers):
        sample = block_index // per_sample
        depth_start = block_index % per_sample * depth_block
        pre_values = (
            apply_weight(gather_taps(padded, row_width), weight) + bias_values[:, None, None, None]
        ).astype(jnp.bfloat16)
        activated = jax.nn.silu(pre_values.astype(jnp.float32))
        if pooled_out:
            result = put_block(
                buffers[1],
                pool_cells(activated, row_width).astype(jnp.bfloat16),
                sample,
                depth_start // 2,
            )
        else:
            result = put_block(buffers[1], activated.astype(jnp.bfloat16), sample, depth_start)
        return (put_block(buffers[0], pre_values, sample, depth_start), result)

    return lax.fori_loop(0, samples * per_sample, forward_block_step, (pre_buffer, out_buffer))


def weight_grads(padded, delta_values, row_width, depth_block, weight):
    samples, depth_total = (delta_values.shape[1], delta_values.shape[2])
    per_sample = depth_total // depth_block
    in_channels = weight.shape[1]

    def weight_block_step(block_index, summed):
        return summed + weight_term(gather_taps(padded, row_width), delta_values, in_channels)

    return lax.fori_loop(
        0, samples * per_sample, weight_block_step, jnp.zeros(weight.shape, jnp.float32)
    )


def data_grads(padded, flipped, row_width, depth_block):
    out_channels = flipped.shape[2]
    samples, depth_total, plane_size = (padded.shape[1], padded.shape[2] - 2, padded.shape[3])
    per_sample = depth_total // depth_block
    out_buffer = jnp.zeros((out_channels, samples, depth_total, plane_size), jnp.bfloat16)

    def data_block_step(block_index, buffer_now):
        sample = block_index // per_sample
        depth_start = block_index % per_sample * depth_block
        result = apply_weight(gather_taps(padded, row_width), flipped).astype(jnp.bfloat16)
        return put_block(buffer_now, result, sample, depth_start)

    return lax.fori_loop(0, samples * per_sample, data_block_step, out_buffer)


def _plane_taps(src_ref, patch_ref, z, row_width):
    channels, _, plane = src_ref.shape
    lane = lax.broadcasted_iota(jnp.int32, (channels, plane), 1)
    row = lane // row_width
    col = lane % row_width
    rows = plane // row_width
    for tap_index in range(27):
        dz = tap_index // 9
        dy = tap_index // 3 % 3 - 1
        dx = tap_index % 3 - 1
        values = src_ref[:, z + dz, :].astype(jnp.float32)
        step = dy * row_width + dx
        if step != 0:
            values = pltpu.roll(values, (-step) % plane, 1)
        valid = (row + dy >= 0) & (row + dy < rows) & (col + dx >= 0) & (col + dx < row_width)
        patch_ref[tap_index * channels : (tap_index + 1) * channels, :] = jnp.where(valid, values, 0.0)

def _forward_kernel(row_width, src_ref, w_ref, b_ref, out_ref, patch_ref):
    for z in range(out_ref.shape[1]):
        _plane_taps(src_ref, patch_ref, z, row_width)
        summed = jnp.dot(w_ref[...], patch_ref[...].astype(jnp.bfloat16), preferred_element_type=jnp.float32)
        out_ref[:, z, :] = (summed + b_ref[...]).astype(out_ref.dtype)

def _grad_kernel(row_width, src_ref, d_ref, out_ref, patch_ref):
    total = jnp.zeros(out_ref.shape, jnp.float32)
    for z in range(d_ref.shape[1]):
        _plane_taps(src_ref, patch_ref, z, row_width)
        total = total + lax.dot_general(
            patch_ref[...].astype(jnp.bfloat16), d_ref[:, z, :],
            (((1,), (1,)), ((), ())), preferred_element_type=jnp.float32)
    out_ref[...] = total

def conv_plane_forward(padded, weight, bias_values, row_width):
    channels, depth, plane = padded.shape
    out_channels = weight.shape[2]
    flat_weight = weight.reshape(27 * channels, out_channels).T
    return pl.pallas_call(
        functools.partial(_forward_kernel, row_width),
        out_shape=jax.ShapeDtypeStruct((out_channels, depth - 2, plane), jnp.bfloat16),
        scratch_shapes=[pltpu.VMEM((27 * channels, plane), jnp.float32)],
    )(padded, flat_weight, bias_values.reshape(out_channels, 1))

def conv_plane_weight_grad(padded, delta, row_width):
    channels, depth, plane = padded.shape
    out_channels = delta.shape[0]
    summed = pl.pallas_call(
        functools.partial(_grad_kernel, row_width),
        out_shape=jax.ShapeDtypeStruct((27 * channels, out_channels), jnp.float32),
        scratch_shapes=[pltpu.VMEM((27 * channels, plane), jnp.float32)],
    )(padded, delta)
    return summed.reshape(27, channels, out_channels)


def bias_sum(delta_values):
    return jnp.sum(delta_values, axis=(1, 2, 3), dtype=jnp.float32)


def per_device(volume, cotangent, w_first, b_first, w_second, b_second, w_third, b_third):
    flipped_second = jnp.flip(w_second, 0).transpose(0, 2, 1)
    flipped_third = jnp.flip(w_third, 0).transpose(0, 2, 1)
    volume_padded = with_halo(volume, (("slab", 2),), 1)
    first_pre = jnp.stack(
        [
            conv_plane_forward(volume_padded[:, s], w_first, b_first, SX)
            for s in range(volume_padded.shape[1])
        ],
        axis=1,
    )
    first_pooled = pool_cells(jax.nn.silu(first_pre.astype(jnp.float32)), SX).astype(jnp.bfloat16)
    first_padded = with_halo(first_pooled, (("slab", 2),), 1)
    second_pre, second_pooled = forward_layer(
        first_padded, w_second, b_second, SX // 2, CZ // 2, True
    )
    coarse_depth = second_pooled.shape[2]
    third_padded = with_halo(second_pooled, (("slab", 2),), 1)
    third_pre, features = forward_layer(
        third_padded, w_third, b_third, SX // 4, coarse_depth, False
    )
    third_delta = (
        cotangent.astype(jnp.float32) * silu_slope(third_pre.astype(jnp.float32))
    ).astype(jnp.bfloat16)
    kernel_third = weight_grads(third_padded, third_delta, SX // 4, coarse_depth, w_third)
    bias_third = bias_sum(third_delta)
    delta_window = with_halo(third_delta, (("slab", 2),), 1)
    second_back = data_grads(delta_window, flipped_third, SX // 4, coarse_depth)
    second_delta = (
        spread_cells(second_back.astype(jnp.float32), SX // 4)
        * silu_slope(second_pre.astype(jnp.float32))
    ).astype(jnp.bfloat16)
    kernel_second = weight_grads(first_padded, second_delta, SX // 2, CZ // 2, w_second)
    bias_second = bias_sum(second_delta)
    delta_padded = with_halo(second_delta, (("slab", 2),), 1)
    first_back = data_grads(delta_padded, flipped_second, SX // 2, CZ // 2)
    first_delta = (
        spread_cells(first_back.astype(jnp.float32), SX // 2)
        * silu_slope(first_pre.astype(jnp.float32))
    ).astype(jnp.bfloat16)
    kernel_first = sum(
        conv_plane_weight_grad(volume_padded[:, s], first_delta[:, s], SX)
        for s in range(volume_padded.shape[1])
    )
    bias_first = bias_sum(first_delta)
    weights = all_reduce_rows(
        (kernel_third, kernel_second, kernel_first, bias_third, bias_second, bias_first)
    )
    kernel_third, kernel_second, kernel_first, bias_third, bias_second, bias_first = weights
    return (
        features,
        kernel_first,
        bias_first,
        kernel_second,
        bias_second,
        kernel_third,
        bias_third,
    )


def xor_pairs(axis, mask):
    return [(i, i ^ mask) for i in range(lax.axis_size(axis))]


def all_reduce_rows(grads, halving_steps=3, lanes=128):
    steps = []
    for axis in ("sample", "slab"):
        mask = 1
        while mask < lax.axis_size(axis):
            steps.append((axis, mask))
            mask *= 2
    pieces, offsets = [], []
    rows = 0
    for g in grads:
        count = -(-g.size // lanes)
        flat = g.reshape(-1)
        flat = jnp.pad(flat, (0, count * lanes - g.size))
        pieces.append(flat.reshape(count, lanes))
        offsets.append(rows)
        rows += count
    block = 8 << halving_steps
    total = -(-rows // block) * block
    if total > rows:
        pieces.append(jnp.zeros((total - rows, lanes), jnp.float32))
    buffer = jnp.concatenate(pieces, axis=0)
    kept = []
    for axis, mask in steps[:halving_steps]:
        half = buffer.shape[0] // 2
        upper = ((lax.axis_index(axis) // mask) % 2).astype(jnp.int32)
        send = lax.dynamic_slice_in_dim(buffer, (1 - upper) * half, half, axis=0)
        keep = lax.dynamic_slice_in_dim(buffer, upper * half, half, axis=0)
        buffer = keep + lax.ppermute(send, axis, xor_pairs(axis, mask))
        kept.append((axis, mask, upper))
    for axis, mask in steps[halving_steps:]:
        buffer = buffer + lax.ppermute(buffer, axis, xor_pairs(axis, mask))
    for axis, mask, upper in reversed(kept):
        other = lax.ppermute(buffer, axis, xor_pairs(axis, mask))
        pair = jnp.stack([buffer, other])
        first = lax.dynamic_index_in_dim(pair, upper, axis=0, keepdims=False)
        second = lax.dynamic_index_in_dim(pair, 1 - upper, axis=0, keepdims=False)
        buffer = jnp.concatenate([first, second], axis=0)
    out = []
    for g, start in zip(grads, offsets):
        count = -(-g.size // lanes)
        part = buffer[start : start + count].reshape(-1)[: g.size]
        out.append(part.reshape(g.shape))
    return tuple(out)


def solution(mesh):
    in_specs = (
        P(None, "sample", "slab", None),
        P(None, "sample", "slab", None),
        P(),
        P(),
        P(),
        P(),
        P(),
        P(),
    )
    out_specs = (P(None, "sample", "slab", None), P(), P(), P(), P(), P(), P())
    return jax.shard_map(
        per_device, mesh=mesh, in_specs=in_specs, out_specs=out_specs, check_vma=False
    )
```

```python
import functools

import jax
import jax.numpy as jnp
from jax import lax
from jax.experimental import pallas as pl
from jax.experimental.pallas import tpu as pltpu
from jax.sharding import PartitionSpec as P

SX = 32
CZ = 4


def with_halo(shard, sides, width):
    for axis, dim in sides:
        size, length = (lax.axis_size(axis), shard.shape[dim])
        up = [(i, (i + 1) % size) for i in range(size - 1)]
        down = [(j, i) for i, j in up]
        last = lax.slice_in_dim(shard, length - width, length, axis=dim)
        first = lax.slice_in_dim(shard, 0, width, axis=dim)
        before = lax.ppermute(last, axis, up)
        after = lax.ppermute(first, axis, down)
        shard = jnp.concatenate([before, shard, after], axis=dim)
    return shard


def silu_slope(values):
    sigmoid = jax.nn.sigmoid(values)
    return sigmoid * (1.0 + values * (1.0 - sigmoid))


def put_block(values, update, sample, depth_start):
    return lax.dynamic_update_slice(values, update, (0, sample, depth_start, 0))


def gather_taps(section, row_width):
    depth_len = section.shape[2] - 2
    plane_size = section.shape[3]
    flattened = jnp.pad(section, ((0, 0), (0, 0), (0, 0), (row_width + 1, row_width + 1)))
    column = lax.broadcasted_iota(jnp.int32, (1, 1, 1, plane_size), 3) % row_width
    left_mask = (column >= 1).astype(section.dtype)
    right_mask = (column <= row_width - 2).astype(section.dtype)
    pieces = []
    for tap_index in range(27):
        depth_start = tap_index // 9
        row_step = tap_index // 3 % 3 - 1
        col_step = tap_index % 3 - 1
        offset = row_width + 1 + row_step * row_width + col_step
        shifted = flattened[
            :, :, depth_start : depth_start + depth_len, offset : offset + plane_size
        ]
        if col_step < 0:
            shifted = shifted * left_mask
        elif col_step > 0:
            shifted = shifted * right_mask
        pieces.append(shifted)
    return jnp.concatenate(pieces, axis=0)


def apply_weight(patches, weight):
    flat_weight = weight.reshape(weight.shape[0] * weight.shape[1], weight.shape[2])
    return jnp.einsum("ko,kgzp->ogzp", flat_weight, patches, preferred_element_type=jnp.float32)


def weight_term(patches, grad_block, in_channels):
    summed = jnp.einsum("kgzp,ogzp->ko", patches, grad_block, preferred_element_type=jnp.float32)
    return summed.reshape(27, in_channels, grad_block.shape[0])


def pool_cells(values, row_width):
    channels, samples, depth_len, plane_size = values.shape
    row_count = plane_size // row_width
    grouped = values.reshape(
        channels, samples, depth_len // 2, 2, row_count // 2, 2, row_width // 2, 2
    )
    return grouped.mean(axis=(3, 5, 7)).reshape(channels, samples, depth_len // 2, plane_size // 4)


def spread_cells(values, coarse_width):
    channels, samples, depth_len, plane_size = values.shape
    row_count = plane_size // coarse_width
    grouped = values.reshape(channels, samples, depth_len, 1, row_count, 1, coarse_width, 1)
    grouped = jnp.broadcast_to(
        grouped, (channels, samples, depth_len, 2, row_count, 2, coarse_width, 2)
    )
    return grouped.reshape(channels, samples, 2 * depth_len, 4 * plane_size) * 0.125


def forward_layer(padded, weight, bias_values, row_width, depth_block, pooled_out):
    out_channels = weight.shape[2]
    samples, depth_total, plane_size = (padded.shape[1], padded.shape[2] - 2, padded.shape[3])
    per_sample = depth_total // depth_block
    pre_buffer = jnp.zeros((out_channels, samples, depth_total, plane_size), jnp.bfloat16)
    if pooled_out:
        out_buffer = jnp.zeros(
            (out_channels, samples, depth_total // 2, plane_size // 4), jnp.bfloat16
        )
    else:
        out_buffer = jnp.zeros_like(pre_buffer)

    def forward_block_step(block_index, buffers):
        sample = block_index // per_sample
        depth_start = block_index % per_sample * depth_block
        pre_values = (
            apply_weight(gather_taps(padded, row_width), weight) + bias_values[:, None, None, None]
        ).astype(jnp.bfloat16)
        activated = jax.nn.silu(pre_values.astype(jnp.float32))
        if pooled_out:
            result = put_block(
                buffers[1],
                pool_cells(activated, row_width).astype(jnp.bfloat16),
                sample,
                depth_start // 2,
            )
        else:
            result = put_block(buffers[1], activated.astype(jnp.bfloat16), sample, depth_start)
        return (put_block(buffers[0], pre_values, sample, depth_start), result)

    return lax.fori_loop(0, samples * per_sample, forward_block_step, (pre_buffer, out_buffer))


def weight_grads(padded, delta_values, row_width, depth_block, weight):
    samples, depth_total = (delta_values.shape[1], delta_values.shape[2])
    per_sample = depth_total // depth_block
    in_channels = weight.shape[1]

    def weight_block_step(block_index, summed):
        return summed + weight_term(gather_taps(padded, row_width), delta_values, in_channels)

    return lax.fori_loop(
        0, samples * per_sample, weight_block_step, jnp.zeros(weight.shape, jnp.float32)
    )


def data_grads(padded, flipped, row_width, depth_block):
    out_channels = flipped.shape[2]
    samples, depth_total, plane_size = (padded.shape[1], padded.shape[2] - 2, padded.shape[3])
    per_sample = depth_total // depth_block
    out_buffer = jnp.zeros((out_channels, samples, depth_total, plane_size), jnp.bfloat16)

    def data_block_step(block_index, buffer_now):
        sample = block_index // per_sample
        depth_start = block_index % per_sample * depth_block
        result = apply_weight(gather_taps(padded, row_width), flipped).astype(jnp.bfloat16)
        return put_block(buffer_now, result, sample, depth_start)

    return lax.fori_loop(0, samples * per_sample, data_block_step, out_buffer)


def _forward_kernel(row_width, src_ref, w_ref, b_ref, out_ref, shifted_ref):
    channels, depth, plane = src_ref.shape
    lane = lax.broadcasted_iota(jnp.int32, (channels, plane), 1)
    row = lane // row_width
    col = lane % row_width
    rows = plane // row_width
    for source_plane in range(depth):
        values = src_ref[:, source_plane, :].astype(jnp.float32)
        for shift_index in range(9):
            dy = shift_index // 3 - 1
            dx = shift_index % 3 - 1
            step = dy * row_width + dx
            moved = pltpu.roll(values, (-step) % plane, 1) if step != 0 else values
            valid = (row + dy >= 0) & (row + dy < rows) & (col + dx >= 0) & (col + dx < row_width)
            shifted_ref[source_plane, shift_index * channels : (shift_index + 1) * channels, :] = (
                jnp.where(valid, moved, 0.0).astype(shifted_ref.dtype)
            )
    for z in range(out_ref.shape[1]):
        summed = b_ref[...] + jnp.zeros((out_ref.shape[0], plane), jnp.float32)
        for dz in range(3):
            summed = summed + jnp.dot(w_ref[dz], shifted_ref[z + dz], preferred_element_type=jnp.float32)
        out_ref[:, z, :] = summed.astype(out_ref.dtype)

def _grad_kernel(shifted_ref, d_ref, out_ref):
    for dz in range(3):
        total = jnp.zeros(out_ref.shape[1:], jnp.float32)
        for z in range(d_ref.shape[1]):
            total = total + lax.dot_general(
                shifted_ref[z + dz], d_ref[:, z, :], (((1,), (1,)), ((), ())),
                preferred_element_type=jnp.float32)
        out_ref[dz] = total

def conv_plane_forward(padded, weight, bias_values, row_width):
    channels, depth, plane = padded.shape
    out_channels = weight.shape[2]
    per_depth = weight.reshape(3, 9 * channels, out_channels).transpose(0, 2, 1)
    return pl.pallas_call(
        functools.partial(_forward_kernel, row_width),
        out_shape=(
            jax.ShapeDtypeStruct((out_channels, depth - 2, plane), jnp.bfloat16),
            jax.ShapeDtypeStruct((depth, 9 * channels, plane), jnp.bfloat16),
        ),
    )(padded, per_depth, bias_values.reshape(out_channels, 1))

def conv_plane_weight_grad(shifted, delta):
    depth, rows, plane = shifted.shape
    out_channels = delta.shape[0]
    summed = pl.pallas_call(
        _grad_kernel,
        out_shape=jax.ShapeDtypeStruct((3, rows, out_channels), jnp.float32),
    )(shifted, delta)
    return summed.reshape(27, rows // 9, out_channels)


def bias_sum(delta_values):
    return jnp.sum(delta_values, axis=(1, 2, 3), dtype=jnp.float32)


def per_device(volume, cotangent, w_first, b_first, w_second, b_second, w_third, b_third):
    flipped_second = jnp.flip(w_second, 0).transpose(0, 2, 1)
    flipped_third = jnp.flip(w_third, 0).transpose(0, 2, 1)
    volume_padded = with_halo(volume, (("slab", 2),), 1)
    first_layer = [
        conv_plane_forward(volume_padded[:, s], w_first, b_first, SX)
        for s in range(volume_padded.shape[1])
    ]
    first_pre = jnp.stack([pre for pre, _ in first_layer], axis=1)
    first_pooled = pool_cells(jax.nn.silu(first_pre.astype(jnp.float32)), SX).astype(jnp.bfloat16)
    first_padded = with_halo(first_pooled, (("slab", 2),), 1)
    second_pre, second_pooled = forward_layer(
        first_padded, w_second, b_second, SX // 2, CZ // 2, True
    )
    coarse_depth = second_pooled.shape[2]
    third_padded = with_halo(second_pooled, (("slab", 2),), 1)
    third_pre, features = forward_layer(
        third_padded, w_third, b_third, SX // 4, coarse_depth, False
    )
    third_delta = (
        cotangent.astype(jnp.float32) * silu_slope(third_pre.astype(jnp.float32))
    ).astype(jnp.bfloat16)
    kernel_third = weight_grads(third_padded, third_delta, SX // 4, coarse_depth, w_third)
    bias_third = bias_sum(third_delta)
    delta_window = with_halo(third_delta, (("slab", 2),), 1)
    second_back = data_grads(delta_window, flipped_third, SX // 4, coarse_depth)
    second_delta = (
        spread_cells(second_back.astype(jnp.float32), SX // 4)
        * silu_slope(second_pre.astype(jnp.float32))
    ).astype(jnp.bfloat16)
    kernel_second = weight_grads(first_padded, second_delta, SX // 2, CZ // 2, w_second)
    bias_second = bias_sum(second_delta)
    delta_padded = with_halo(second_delta, (("slab", 2),), 1)
    first_back = data_grads(delta_padded, flipped_second, SX // 2, CZ // 2)
    first_delta = (
        spread_cells(first_back.astype(jnp.float32), SX // 2)
        * silu_slope(first_pre.astype(jnp.float32))
    ).astype(jnp.bfloat16)
    kernel_first = sum(
        conv_plane_weight_grad(shifted, first_delta[:, s])
        for s, (_, shifted) in enumerate(first_layer)
    )
    bias_first = bias_sum(first_delta)
    weights = all_reduce_rows(
        (kernel_third, kernel_second, kernel_first, bias_third, bias_second, bias_first)
    )
    kernel_third, kernel_second, kernel_first, bias_third, bias_second, bias_first = weights
    return (
        features,
        kernel_first,
        bias_first,
        kernel_second,
        bias_second,
        kernel_third,
        bias_third,
    )


def xor_pairs(axis, mask):
    return [(i, i ^ mask) for i in range(lax.axis_size(axis))]


def all_reduce_rows(grads, halving_steps=3, lanes=128):
    steps = []
    for axis in ("sample", "slab"):
        mask = 1
        while mask < lax.axis_size(axis):
            steps.append((axis, mask))
            mask *= 2
    pieces, offsets = [], []
    rows = 0
    for g in grads:
        count = -(-g.size // lanes)
        flat = g.reshape(-1)
        flat = jnp.pad(flat, (0, count * lanes - g.size))
        pieces.append(flat.reshape(count, lanes))
        offsets.append(rows)
        rows += count
    block = 8 << halving_steps
    total = -(-rows // block) * block
    if total > rows:
        pieces.append(jnp.zeros((total - rows, lanes), jnp.float32))
    buffer = jnp.concatenate(pieces, axis=0)
    kept = []
    for axis, mask in steps[:halving_steps]:
        half = buffer.shape[0] // 2
        upper = ((lax.axis_index(axis) // mask) % 2).astype(jnp.int32)
        send = lax.dynamic_slice_in_dim(buffer, (1 - upper) * half, half, axis=0)
        keep = lax.dynamic_slice_in_dim(buffer, upper * half, half, axis=0)
        buffer = keep + lax.ppermute(send, axis, xor_pairs(axis, mask))
        kept.append((axis, mask, upper))
    for axis, mask in steps[halving_steps:]:
        buffer = buffer + lax.ppermute(buffer, axis, xor_pairs(axis, mask))
    for axis, mask, upper in reversed(kept):
        other = lax.ppermute(buffer, axis, xor_pairs(axis, mask))
        pair = jnp.stack([buffer, other])
        first = lax.dynamic_index_in_dim(pair, upper, axis=0, keepdims=False)
        second = lax.dynamic_index_in_dim(pair, 1 - upper, axis=0, keepdims=False)
        buffer = jnp.concatenate([first, second], axis=0)
    out = []
    for g, start in zip(grads, offsets):
        count = -(-g.size // lanes)
        part = buffer[start : start + count].reshape(-1)[: g.size]
        out.append(part.reshape(g.shape))
    return tuple(out)


def solution(mesh):
    in_specs = (
        P(None, "sample", "slab", None),
        P(None, "sample", "slab", None),
        P(),
        P(),
        P(),
        P(),
        P(),
        P(),
    )
    out_specs = (P(None, "sample", "slab", None), P(), P(), P(), P(), P(), P())
    return jax.shard_map(
        per_device, mesh=mesh, in_specs=in_specs, out_specs=out_specs, check_vma=False
    )
```

```python
import functools

import jax
import jax.numpy as jnp
from jax import lax
from jax.experimental import pallas as pl
from jax.experimental.pallas import tpu as pltpu
from jax.sharding import PartitionSpec as P

SX = 32
CZ = 4


def with_halo(shard, sides, width):
    for axis, dim in sides:
        size, length = (lax.axis_size(axis), shard.shape[dim])
        up = [(i, (i + 1) % size) for i in range(size - 1)]
        down = [(j, i) for i, j in up]
        last = lax.slice_in_dim(shard, length - width, length, axis=dim)
        first = lax.slice_in_dim(shard, 0, width, axis=dim)
        before = lax.ppermute(last, axis, up)
        after = lax.ppermute(first, axis, down)
        shard = jnp.concatenate([before, shard, after], axis=dim)
    return shard


def silu_slope(values):
    sigmoid = jax.nn.sigmoid(values)
    return sigmoid * (1.0 + values * (1.0 - sigmoid))


def put_block(values, update, sample, depth_start):
    return lax.dynamic_update_slice(values, update, (0, sample, depth_start, 0))


def gather_taps(section, row_width):
    depth_len = section.shape[2] - 2
    plane_size = section.shape[3]
    flattened = jnp.pad(section, ((0, 0), (0, 0), (0, 0), (row_width + 1, row_width + 1)))
    column = lax.broadcasted_iota(jnp.int32, (1, 1, 1, plane_size), 3) % row_width
    left_mask = (column >= 1).astype(section.dtype)
    right_mask = (column <= row_width - 2).astype(section.dtype)
    pieces = []
    for tap_index in range(27):
        depth_start = tap_index // 9
        row_step = tap_index // 3 % 3 - 1
        col_step = tap_index % 3 - 1
        offset = row_width + 1 + row_step * row_width + col_step
        shifted = flattened[
            :, :, depth_start : depth_start + depth_len, offset : offset + plane_size
        ]
        if col_step < 0:
            shifted = shifted * left_mask
        elif col_step > 0:
            shifted = shifted * right_mask
        pieces.append(shifted)
    return jnp.concatenate(pieces, axis=0)


def apply_weight(patches, weight):
    flat_weight = weight.reshape(weight.shape[0] * weight.shape[1], weight.shape[2])
    return jnp.einsum("ko,kgzp->ogzp", flat_weight, patches, preferred_element_type=jnp.float32)


def weight_term(patches, grad_block, in_channels):
    summed = jnp.einsum("kgzp,ogzp->ko", patches, grad_block, preferred_element_type=jnp.float32)
    return summed.reshape(27, in_channels, grad_block.shape[0])


def pool_cells(values, row_width):
    channels, samples, depth_len, plane_size = values.shape
    row_count = plane_size // row_width
    grouped = values.reshape(
        channels, samples, depth_len // 2, 2, row_count // 2, 2, row_width // 2, 2
    )
    return grouped.mean(axis=(3, 5, 7)).reshape(channels, samples, depth_len // 2, plane_size // 4)


def spread_cells(values, coarse_width):
    channels, samples, depth_len, plane_size = values.shape
    row_count = plane_size // coarse_width
    grouped = values.reshape(channels, samples, depth_len, 1, row_count, 1, coarse_width, 1)
    grouped = jnp.broadcast_to(
        grouped, (channels, samples, depth_len, 2, row_count, 2, coarse_width, 2)
    )
    return grouped.reshape(channels, samples, 2 * depth_len, 4 * plane_size) * 0.125


def forward_layer(padded, weight, bias_values, row_width, depth_block, pooled_out):
    out_channels = weight.shape[2]
    samples, depth_total, plane_size = (padded.shape[1], padded.shape[2] - 2, padded.shape[3])
    per_sample = depth_total // depth_block
    pre_buffer = jnp.zeros((out_channels, samples, depth_total, plane_size), jnp.bfloat16)
    if pooled_out:
        out_buffer = jnp.zeros(
            (out_channels, samples, depth_total // 2, plane_size // 4), jnp.bfloat16
        )
    else:
        out_buffer = jnp.zeros_like(pre_buffer)

    def forward_block_step(block_index, buffers):
        sample = block_index // per_sample
        depth_start = block_index % per_sample * depth_block
        pre_values = (
            apply_weight(gather_taps(padded, row_width), weight) + bias_values[:, None, None, None]
        ).astype(jnp.bfloat16)
        activated = jax.nn.silu(pre_values.astype(jnp.float32))
        if pooled_out:
            result = put_block(
                buffers[1],
                pool_cells(activated, row_width).astype(jnp.bfloat16),
                sample,
                depth_start // 2,
            )
        else:
            result = put_block(buffers[1], activated.astype(jnp.bfloat16), sample, depth_start)
        return (put_block(buffers[0], pre_values, sample, depth_start), result)

    return lax.fori_loop(0, samples * per_sample, forward_block_step, (pre_buffer, out_buffer))


def weight_grads(padded, delta_values, row_width, depth_block, weight):
    samples, depth_total = (delta_values.shape[1], delta_values.shape[2])
    per_sample = depth_total // depth_block
    in_channels = weight.shape[1]

    def weight_block_step(block_index, summed):
        return summed + weight_term(gather_taps(padded, row_width), delta_values, in_channels)

    return lax.fori_loop(
        0, samples * per_sample, weight_block_step, jnp.zeros(weight.shape, jnp.float32)
    )


def data_grads(padded, flipped, row_width, depth_block):
    out_channels = flipped.shape[2]
    samples, depth_total, plane_size = (padded.shape[1], padded.shape[2] - 2, padded.shape[3])
    per_sample = depth_total // depth_block
    out_buffer = jnp.zeros((out_channels, samples, depth_total, plane_size), jnp.bfloat16)

    def data_block_step(block_index, buffer_now):
        sample = block_index // per_sample
        depth_start = block_index % per_sample * depth_block
        result = apply_weight(gather_taps(padded, row_width), flipped).astype(jnp.bfloat16)
        return put_block(buffer_now, result, sample, depth_start)

    return lax.fori_loop(0, samples * per_sample, data_block_step, out_buffer)


def parity_split(values, row_width):
    c, n, z, plane = values.shape
    rows = plane // row_width
    grouped = values.reshape(c, n, z, rows // 2, 2, row_width // 2, 2)
    grouped = grouped.transpose(0, 1, 2, 4, 6, 3, 5)
    return grouped.reshape(c, n, z, 4, plane // 4)

def parity_taps(split, coarse_width):
    depth_len = split.shape[2] - 2
    size = split.shape[4]
    pad = coarse_width + 1
    flattened = jnp.pad(split, ((0, 0), (0, 0), (0, 0), (0, 0), (pad, pad)))
    column = lax.broadcasted_iota(jnp.int32, (1, 1, 1, size), 3) % coarse_width
    left_mask = (column >= 1).astype(split.dtype)
    right_mask = (column <= coarse_width - 2).astype(split.dtype)
    blocks = []
    for a in range(2):
        for b in range(2):
            pieces = []
            for tap_index in range(27):
                depth_start = tap_index // 9
                row_sum = a + tap_index // 3 % 3 - 1
                col_sum = b + tap_index % 3 - 1
                source = (row_sum % 2) * 2 + col_sum % 2
                row_step, col_step = row_sum // 2, col_sum // 2
                offset = pad + row_step * coarse_width + col_step
                shifted = flattened[:, :, depth_start : depth_start + depth_len, source, offset : offset + size]
                if col_step < 0:
                    shifted = shifted * left_mask
                elif col_step > 0:
                    shifted = shifted * right_mask
                pieces.append(shifted)
            blocks.append(jnp.concatenate(pieces, axis=0))
    return jnp.stack(blocks, axis=3)

def parity_pool(values):
    c, n, z, parities, size = values.shape
    return values.reshape(c, n, z // 2, 2 * parities, size).mean(axis=3)

def parity_spread(values):
    c, n, z, size = values.shape
    grouped = jnp.broadcast_to(values[:, :, :, None, None, :], (c, n, z, 2, 4, size))
    return grouped.reshape(c, n, 2 * z, 4, size) * 0.125


def _parity_kernel(coarse_width, src_ref, w_ref, b_ref, out_ref, shifted_ref):
    channels, depth, _, size = src_ref.shape
    lane = lax.broadcasted_iota(jnp.int32, (channels, size), 1)
    row = lane // coarse_width
    col = lane % coarse_width
    rows = size // coarse_width
    for source_plane in range(depth):
        cache = {}
        for a in range(2):
            for b in range(2):
                for shift_index in range(9):
                    row_sum = a + shift_index // 3 - 1
                    col_sum = b + shift_index % 3 - 1
                    key = (row_sum % 2, col_sum % 2, row_sum // 2, col_sum // 2)
                    if key not in cache:
                        source, row_step, col_step = key[0] * 2 + key[1], key[2], key[3]
                        values = src_ref[:, source_plane, source, :].astype(jnp.float32)
                        step = row_step * coarse_width + col_step
                        if step != 0:
                            values = pltpu.roll(values, (-step) % size, 1)
                        valid = (
                            (row + row_step >= 0) & (row + row_step < rows)
                            & (col + col_step >= 0) & (col + col_step < coarse_width)
                        )
                        cache[key] = jnp.where(valid, values, 0.0).astype(shifted_ref.dtype)
                    shifted_ref[source_plane, a * 2 + b, shift_index * channels : (shift_index + 1) * channels, :] = cache[key]
    for z in range(out_ref.shape[1]):
        for parity in range(4):
            summed = b_ref[...] + jnp.zeros((out_ref.shape[0], size), jnp.float32)
            for dz in range(3):
                summed = summed + jnp.dot(
                    w_ref[dz], shifted_ref[z + dz, parity], preferred_element_type=jnp.float32
                )
            out_ref[:, z, parity, :] = summed.astype(out_ref.dtype)

def parity_conv_forward(split, weight, bias_values, coarse_width):
    channels, depth, parities, size = split.shape
    out_channels = weight.shape[2]
    per_depth = weight.reshape(3, 9 * channels, out_channels).transpose(0, 2, 1)
    return pl.pallas_call(
        functools.partial(_parity_kernel, coarse_width),
        out_shape=(
            jax.ShapeDtypeStruct((out_channels, depth - 2, parities, size), jnp.bfloat16),
            jax.ShapeDtypeStruct((depth, parities, 9 * channels, size), jnp.bfloat16),
        ),
    )(split, per_depth, bias_values.reshape(out_channels, 1))

def parity_weight_grad(shifted, delta):
    depth_len = delta.shape[1]
    per_depth = [
        jnp.einsum(
            "zpkq,ozpq->ko", shifted[dz : dz + depth_len], delta, preferred_element_type=jnp.float32
        )
        for dz in range(3)
    ]
    return jnp.stack(per_depth).reshape(27, shifted.shape[2] // 9, delta.shape[0])


def bias_sum(delta_values):
    return jnp.sum(delta_values, axis=(1, 2, 3), dtype=jnp.float32)


def per_device(volume, cotangent, w_first, b_first, w_second, b_second, w_third, b_third):
    flipped_second = jnp.flip(w_second, 0).transpose(0, 2, 1)
    flipped_third = jnp.flip(w_third, 0).transpose(0, 2, 1)
    volume_padded = with_halo(volume, (("slab", 2),), 1)
    first_split = parity_split(volume_padded, SX)
    first_layer = [
        parity_conv_forward(first_split[:, s], w_first, b_first, SX // 2)
        for s in range(first_split.shape[1])
    ]
    first_pre = jnp.stack([pre for pre, _ in first_layer], axis=1)
    first_pooled = parity_pool(jax.nn.silu(first_pre.astype(jnp.float32))).astype(jnp.bfloat16)
    first_padded = with_halo(first_pooled, (("slab", 2),), 1)
    second_pre, second_pooled = forward_layer(
        first_padded, w_second, b_second, SX // 2, CZ // 2, True
    )
    coarse_depth = second_pooled.shape[2]
    third_padded = with_halo(second_pooled, (("slab", 2),), 1)
    third_pre, features = forward_layer(
        third_padded, w_third, b_third, SX // 4, coarse_depth, False
    )
    third_delta = (
        cotangent.astype(jnp.float32) * silu_slope(third_pre.astype(jnp.float32))
    ).astype(jnp.bfloat16)
    kernel_third = weight_grads(third_padded, third_delta, SX // 4, coarse_depth, w_third)
    bias_third = bias_sum(third_delta)
    delta_window = with_halo(third_delta, (("slab", 2),), 1)
    second_back = data_grads(delta_window, flipped_third, SX // 4, coarse_depth)
    second_delta = (
        spread_cells(second_back.astype(jnp.float32), SX // 4)
        * silu_slope(second_pre.astype(jnp.float32))
    ).astype(jnp.bfloat16)
    kernel_second = weight_grads(first_padded, second_delta, SX // 2, CZ // 2, w_second)
    bias_second = bias_sum(second_delta)
    delta_padded = with_halo(second_delta, (("slab", 2),), 1)
    first_back = data_grads(delta_padded, flipped_second, SX // 2, CZ // 2)
    first_delta = (
        parity_spread(first_back.astype(jnp.float32)) * silu_slope(first_pre.astype(jnp.float32))
    ).astype(jnp.bfloat16)
    kernel_first = sum(
        parity_weight_grad(shifted, first_delta[:, s])
        for s, (_, shifted) in enumerate(first_layer)
    )
    bias_first = jnp.sum(first_delta, axis=(1, 2, 3, 4), dtype=jnp.float32)
    weights = all_reduce_rows(
        (kernel_third, kernel_second, kernel_first, bias_third, bias_second, bias_first)
    )
    kernel_third, kernel_second, kernel_first, bias_third, bias_second, bias_first = weights
    return (
        features,
        kernel_first,
        bias_first,
        kernel_second,
        bias_second,
        kernel_third,
        bias_third,
    )


def xor_pairs(axis, mask):
    return [(i, i ^ mask) for i in range(lax.axis_size(axis))]


def all_reduce_rows(grads, halving_steps=3, lanes=128):
    steps = []
    for axis in ("sample", "slab"):
        mask = 1
        while mask < lax.axis_size(axis):
            steps.append((axis, mask))
            mask *= 2
    pieces, offsets = [], []
    rows = 0
    for g in grads:
        count = -(-g.size // lanes)
        flat = g.reshape(-1)
        flat = jnp.pad(flat, (0, count * lanes - g.size))
        pieces.append(flat.reshape(count, lanes))
        offsets.append(rows)
        rows += count
    block = 8 << halving_steps
    total = -(-rows // block) * block
    if total > rows:
        pieces.append(jnp.zeros((total - rows, lanes), jnp.float32))
    buffer = jnp.concatenate(pieces, axis=0)
    kept = []
    for axis, mask in steps[:halving_steps]:
        half = buffer.shape[0] // 2
        upper = ((lax.axis_index(axis) // mask) % 2).astype(jnp.int32)
        send = lax.dynamic_slice_in_dim(buffer, (1 - upper) * half, half, axis=0)
        keep = lax.dynamic_slice_in_dim(buffer, upper * half, half, axis=0)
        buffer = keep + lax.ppermute(send, axis, xor_pairs(axis, mask))
        kept.append((axis, mask, upper))
    for axis, mask in steps[halving_steps:]:
        buffer = buffer + lax.ppermute(buffer, axis, xor_pairs(axis, mask))
    for axis, mask, upper in reversed(kept):
        other = lax.ppermute(buffer, axis, xor_pairs(axis, mask))
        pair = jnp.stack([buffer, other])
        first = lax.dynamic_index_in_dim(pair, upper, axis=0, keepdims=False)
        second = lax.dynamic_index_in_dim(pair, 1 - upper, axis=0, keepdims=False)
        buffer = jnp.concatenate([first, second], axis=0)
    out = []
    for g, start in zip(grads, offsets):
        count = -(-g.size // lanes)
        part = buffer[start : start + count].reshape(-1)[: g.size]
        out.append(part.reshape(g.shape))
    return tuple(out)


def solution(mesh):
    in_specs = (
        P(None, "sample", "slab", None),
        P(None, "sample", "slab", None),
        P(),
        P(),
        P(),
        P(),
        P(),
        P(),
    )
    out_specs = (P(None, "sample", "slab", None), P(), P(), P(), P(), P(), P())
    return jax.shard_map(
        per_device, mesh=mesh, in_specs=in_specs, out_specs=out_specs, check_vma=False
    )
```

```python
import functools

import jax
import jax.numpy as jnp
from jax import lax
from jax.experimental import pallas as pl
from jax.experimental.pallas import tpu as pltpu
from jax.sharding import PartitionSpec as P

SX = 32
CZ = 4


def with_halo(shard, sides, width):
    for axis, dim in sides:
        size, length = (lax.axis_size(axis), shard.shape[dim])
        up = [(i, (i + 1) % size) for i in range(size - 1)]
        down = [(j, i) for i, j in up]
        last = lax.slice_in_dim(shard, length - width, length, axis=dim)
        first = lax.slice_in_dim(shard, 0, width, axis=dim)
        before = lax.ppermute(last, axis, up)
        after = lax.ppermute(first, axis, down)
        shard = jnp.concatenate([before, shard, after], axis=dim)
    return shard


def silu_slope(values):
    sigmoid = jax.nn.sigmoid(values)
    return sigmoid * (1.0 + values * (1.0 - sigmoid))


def put_block(values, update, sample, depth_start):
    return lax.dynamic_update_slice(values, update, (0, sample, depth_start, 0))


def gather_taps(section, row_width):
    depth_len = section.shape[2] - 2
    plane_size = section.shape[3]
    flattened = jnp.pad(section, ((0, 0), (0, 0), (0, 0), (row_width + 1, row_width + 1)))
    column = lax.broadcasted_iota(jnp.int32, (1, 1, 1, plane_size), 3) % row_width
    left_mask = (column >= 1).astype(section.dtype)
    right_mask = (column <= row_width - 2).astype(section.dtype)
    pieces = []
    for tap_index in range(27):
        depth_start = tap_index // 9
        row_step = tap_index // 3 % 3 - 1
        col_step = tap_index % 3 - 1
        offset = row_width + 1 + row_step * row_width + col_step
        shifted = flattened[
            :, :, depth_start : depth_start + depth_len, offset : offset + plane_size
        ]
        if col_step < 0:
            shifted = shifted * left_mask
        elif col_step > 0:
            shifted = shifted * right_mask
        pieces.append(shifted)
    return jnp.concatenate(pieces, axis=0)


def apply_weight(patches, weight):
    flat_weight = weight.reshape(weight.shape[0] * weight.shape[1], weight.shape[2])
    return jnp.einsum("ko,kgzp->ogzp", flat_weight, patches, preferred_element_type=jnp.float32)


def weight_term(patches, grad_block, in_channels):
    summed = jnp.einsum("kgzp,ogzp->ko", patches, grad_block, preferred_element_type=jnp.float32)
    return summed.reshape(27, in_channels, grad_block.shape[0])


def pool_cells(values, row_width):
    channels, samples, depth_len, plane_size = values.shape
    row_count = plane_size // row_width
    grouped = values.reshape(
        channels, samples, depth_len // 2, 2, row_count // 2, 2, row_width // 2, 2
    )
    return grouped.mean(axis=(3, 5, 7)).reshape(channels, samples, depth_len // 2, plane_size // 4)


def spread_cells(values, coarse_width):
    channels, samples, depth_len, plane_size = values.shape
    row_count = plane_size // coarse_width
    grouped = values.reshape(channels, samples, depth_len, 1, row_count, 1, coarse_width, 1)
    grouped = jnp.broadcast_to(
        grouped, (channels, samples, depth_len, 2, row_count, 2, coarse_width, 2)
    )
    return grouped.reshape(channels, samples, 2 * depth_len, 4 * plane_size) * 0.125


def forward_layer(padded, weight, bias_values, row_width, depth_block, pooled_out):
    out_channels = weight.shape[2]
    samples, depth_total, plane_size = (padded.shape[1], padded.shape[2] - 2, padded.shape[3])
    per_sample = depth_total // depth_block
    pre_buffer = jnp.zeros((out_channels, samples, depth_total, plane_size), jnp.bfloat16)
    if pooled_out:
        out_buffer = jnp.zeros(
            (out_channels, samples, depth_total // 2, plane_size // 4), jnp.bfloat16
        )
    else:
        out_buffer = jnp.zeros_like(pre_buffer)

    def forward_block_step(block_index, buffers):
        sample = block_index // per_sample
        depth_start = block_index % per_sample * depth_block
        pre_values = (
            apply_weight(gather_taps(padded, row_width), weight) + bias_values[:, None, None, None]
        ).astype(jnp.bfloat16)
        activated = jax.nn.silu(pre_values.astype(jnp.float32))
        if pooled_out:
            result = put_block(
                buffers[1],
                pool_cells(activated, row_width).astype(jnp.bfloat16),
                sample,
                depth_start // 2,
            )
        else:
            result = put_block(buffers[1], activated.astype(jnp.bfloat16), sample, depth_start)
        return (put_block(buffers[0], pre_values, sample, depth_start), result)

    return lax.fori_loop(0, samples * per_sample, forward_block_step, (pre_buffer, out_buffer))


def weight_grads(padded, delta_values, row_width, depth_block, weight):
    samples, depth_total = (delta_values.shape[1], delta_values.shape[2])
    per_sample = depth_total // depth_block
    in_channels = weight.shape[1]

    def weight_block_step(block_index, summed):
        return summed + weight_term(gather_taps(padded, row_width), delta_values, in_channels)

    return lax.fori_loop(
        0, samples * per_sample, weight_block_step, jnp.zeros(weight.shape, jnp.float32)
    )


def data_grads(padded, flipped, row_width, depth_block):
    out_channels = flipped.shape[2]
    samples, depth_total, plane_size = (padded.shape[1], padded.shape[2] - 2, padded.shape[3])
    per_sample = depth_total // depth_block
    out_buffer = jnp.zeros((out_channels, samples, depth_total, plane_size), jnp.bfloat16)

    def data_block_step(block_index, buffer_now):
        sample = block_index // per_sample
        depth_start = block_index % per_sample * depth_block
        result = apply_weight(gather_taps(padded, row_width), flipped).astype(jnp.bfloat16)
        return put_block(buffer_now, result, sample, depth_start)

    return lax.fori_loop(0, samples * per_sample, data_block_step, out_buffer)


def parity_pool(values):
    c, n, z, parities, size = values.shape
    return values.reshape(c, n, z // 2, 2 * parities, size).mean(axis=3)

def parity_spread(values):
    c, n, z, size = values.shape
    grouped = jnp.broadcast_to(values[:, :, :, None, None, :], (c, n, z, 2, 4, size))
    return grouped.reshape(c, n, 2 * z, 4, size) * 0.125


def parity_permutation(row_width, chunk=128):
    lane = jnp.arange(chunk)
    yy, x = lane // row_width, lane % row_width
    target = ((yy % 2) * 2 + x % 2) * (chunk // 4) + (yy // 2) * (row_width // 2) + x // 2
    return (target[:, None] == jnp.arange(chunk)[None, :]).astype(jnp.bfloat16)

def _parity_kernel(coarse_width, channels, src_ref, perm_ref, w_ref, b_ref, out_ref, shifted_ref, sub_ref):
    rows_total, plane = src_ref.shape
    depth = rows_total // channels
    chunk = perm_ref.shape[0]
    quarter = chunk // 4
    for g in range(plane // chunk):
        moved = jnp.dot(src_ref[:, g * chunk : (g + 1) * chunk], perm_ref[...], preferred_element_type=jnp.float32)
        for s in range(4):
            sub_ref[s, :, g * quarter : (g + 1) * quarter] = moved[:, s * quarter : (s + 1) * quarter]
    size = plane // 4
    lane = lax.broadcasted_iota(jnp.int32, (channels, size), 1)
    row = lane // coarse_width
    col = lane % coarse_width
    rows = size // coarse_width
    for source_plane in range(depth):
        cache = {}
        for a in range(2):
            for b in range(2):
                for shift_index in range(9):
                    row_sum = a + shift_index // 3 - 1
                    col_sum = b + shift_index % 3 - 1
                    key = (row_sum % 2, col_sum % 2, row_sum // 2, col_sum // 2)
                    if key not in cache:
                        source, row_step, col_step = key[0] * 2 + key[1], key[2], key[3]
                        values = sub_ref[source, source_plane * channels : (source_plane + 1) * channels, :]
                        step = row_step * coarse_width + col_step
                        if step != 0:
                            values = pltpu.roll(values, (-step) % size, 1)
                        valid = (
                            (row + row_step >= 0) & (row + row_step < rows)
                            & (col + col_step >= 0) & (col + col_step < coarse_width)
                        )
                        cache[key] = jnp.where(valid, values, 0.0).astype(shifted_ref.dtype)
                    shifted_ref[source_plane, a * 2 + b, shift_index * channels : (shift_index + 1) * channels, :] = cache[key]
    for z in range(out_ref.shape[1]):
        for parity in range(4):
            summed = b_ref[...] + jnp.zeros((out_ref.shape[0], size), jnp.float32)
            for dz in range(3):
                summed = summed + jnp.dot(
                    w_ref[dz], shifted_ref[z + dz, parity], preferred_element_type=jnp.float32
                )
            out_ref[:, z, parity, :] = summed.astype(out_ref.dtype)

def parity_conv_forward(padded, weight, bias_values, row_width):
    channels, depth, plane = padded.shape
    out_channels = weight.shape[2]
    per_depth = weight.reshape(3, 9 * channels, out_channels).transpose(0, 2, 1)
    by_plane = padded.transpose(1, 0, 2).reshape(depth * channels, plane)
    return pl.pallas_call(
        functools.partial(_parity_kernel, row_width // 2, channels),
        out_shape=(
            jax.ShapeDtypeStruct((out_channels, depth - 2, 4, plane // 4), jnp.bfloat16),
            jax.ShapeDtypeStruct((depth, 4, 9 * channels, plane // 4), jnp.bfloat16),
        ),
        scratch_shapes=[pltpu.VMEM((4, depth * channels, plane // 4), jnp.float32)],
    )(by_plane, parity_permutation(row_width), per_depth, bias_values.reshape(out_channels, 1))


def parity_weight_grad(shifted, delta):
    depth_len = delta.shape[1]
    per_depth = [
        jnp.einsum(
            "zpkq,ozpq->ko", shifted[dz : dz + depth_len], delta, preferred_element_type=jnp.float32
        )
        for dz in range(3)
    ]
    return jnp.stack(per_depth).reshape(27, shifted.shape[2] // 9, delta.shape[0])


def bias_sum(delta_values):
    return jnp.sum(delta_values, axis=(1, 2, 3), dtype=jnp.float32)


def per_device(volume, cotangent, w_first, b_first, w_second, b_second, w_third, b_third):
    flipped_second = jnp.flip(w_second, 0).transpose(0, 2, 1)
    flipped_third = jnp.flip(w_third, 0).transpose(0, 2, 1)
    volume_padded = with_halo(volume, (("slab", 2),), 1)
    first_layer = [
        parity_conv_forward(volume_padded[:, s], w_first, b_first, SX)
        for s in range(volume_padded.shape[1])
    ]
    first_pre = jnp.stack([pre for pre, _ in first_layer], axis=1)
    first_pooled = parity_pool(jax.nn.silu(first_pre.astype(jnp.float32))).astype(jnp.bfloat16)
    first_padded = with_halo(first_pooled, (("slab", 2),), 1)
    second_pre, second_pooled = forward_layer(
        first_padded, w_second, b_second, SX // 2, CZ // 2, True
    )
    coarse_depth = second_pooled.shape[2]
    third_padded = with_halo(second_pooled, (("slab", 2),), 1)
    third_pre, features = forward_layer(
        third_padded, w_third, b_third, SX // 4, coarse_depth, False
    )
    third_delta = (
        cotangent.astype(jnp.float32) * silu_slope(third_pre.astype(jnp.float32))
    ).astype(jnp.bfloat16)
    kernel_third = weight_grads(third_padded, third_delta, SX // 4, coarse_depth, w_third)
    bias_third = bias_sum(third_delta)
    delta_window = with_halo(third_delta, (("slab", 2),), 1)
    second_back = data_grads(delta_window, flipped_third, SX // 4, coarse_depth)
    second_delta = (
        spread_cells(second_back.astype(jnp.float32), SX // 4)
        * silu_slope(second_pre.astype(jnp.float32))
    ).astype(jnp.bfloat16)
    kernel_second = weight_grads(first_padded, second_delta, SX // 2, CZ // 2, w_second)
    bias_second = bias_sum(second_delta)
    delta_padded = with_halo(second_delta, (("slab", 2),), 1)
    first_back = data_grads(delta_padded, flipped_second, SX // 2, CZ // 2)
    first_delta = (
        parity_spread(first_back.astype(jnp.float32)) * silu_slope(first_pre.astype(jnp.float32))
    ).astype(jnp.bfloat16)
    kernel_first = sum(
        parity_weight_grad(shifted, first_delta[:, s])
        for s, (_, shifted) in enumerate(first_layer)
    )
    bias_first = jnp.sum(first_delta, axis=(1, 2, 3, 4), dtype=jnp.float32)
    weights = all_reduce_rows(
        (kernel_third, kernel_second, kernel_first, bias_third, bias_second, bias_first)
    )
    kernel_third, kernel_second, kernel_first, bias_third, bias_second, bias_first = weights
    return (
        features,
        kernel_first,
        bias_first,
        kernel_second,
        bias_second,
        kernel_third,
        bias_third,
    )


def xor_pairs(axis, mask):
    return [(i, i ^ mask) for i in range(lax.axis_size(axis))]


def all_reduce_rows(grads, halving_steps=3, lanes=128):
    steps = []
    for axis in ("sample", "slab"):
        mask = 1
        while mask < lax.axis_size(axis):
            steps.append((axis, mask))
            mask *= 2
    pieces, offsets = [], []
    rows = 0
    for g in grads:
        count = -(-g.size // lanes)
        flat = g.reshape(-1)
        flat = jnp.pad(flat, (0, count * lanes - g.size))
        pieces.append(flat.reshape(count, lanes))
        offsets.append(rows)
        rows += count
    block = 8 << halving_steps
    total = -(-rows // block) * block
    if total > rows:
        pieces.append(jnp.zeros((total - rows, lanes), jnp.float32))
    buffer = jnp.concatenate(pieces, axis=0)
    kept = []
    for axis, mask in steps[:halving_steps]:
        half = buffer.shape[0] // 2
        upper = ((lax.axis_index(axis) // mask) % 2).astype(jnp.int32)
        send = lax.dynamic_slice_in_dim(buffer, (1 - upper) * half, half, axis=0)
        keep = lax.dynamic_slice_in_dim(buffer, upper * half, half, axis=0)
        buffer = keep + lax.ppermute(send, axis, xor_pairs(axis, mask))
        kept.append((axis, mask, upper))
    for axis, mask in steps[halving_steps:]:
        buffer = buffer + lax.ppermute(buffer, axis, xor_pairs(axis, mask))
    for axis, mask, upper in reversed(kept):
        other = lax.ppermute(buffer, axis, xor_pairs(axis, mask))
        pair = jnp.stack([buffer, other])
        first = lax.dynamic_index_in_dim(pair, upper, axis=0, keepdims=False)
        second = lax.dynamic_index_in_dim(pair, 1 - upper, axis=0, keepdims=False)
        buffer = jnp.concatenate([first, second], axis=0)
    out = []
    for g, start in zip(grads, offsets):
        count = -(-g.size // lanes)
        part = buffer[start : start + count].reshape(-1)[: g.size]
        out.append(part.reshape(g.shape))
    return tuple(out)


def solution(mesh):
    in_specs = (
        P(None, "sample", "slab", None),
        P(None, "sample", "slab", None),
        P(),
        P(),
        P(),
        P(),
        P(),
        P(),
    )
    out_specs = (P(None, "sample", "slab", None), P(), P(), P(), P(), P(), P())
    return jax.shard_map(
        per_device, mesh=mesh, in_specs=in_specs, out_specs=out_specs, check_vma=False
    )
```

```python
import functools

import jax
import jax.numpy as jnp
from jax import lax
from jax.experimental import pallas as pl
from jax.experimental.pallas import tpu as pltpu
from jax.sharding import PartitionSpec as P

SX = 32
CZ = 4


def with_halo(shard, sides, width):
    for axis, dim in sides:
        size, length = (lax.axis_size(axis), shard.shape[dim])
        up = [(i, (i + 1) % size) for i in range(size - 1)]
        down = [(j, i) for i, j in up]
        last = lax.slice_in_dim(shard, length - width, length, axis=dim)
        first = lax.slice_in_dim(shard, 0, width, axis=dim)
        before = lax.ppermute(last, axis, up)
        after = lax.ppermute(first, axis, down)
        shard = jnp.concatenate([before, shard, after], axis=dim)
    return shard


def silu_slope(values):
    sigmoid = jax.nn.sigmoid(values)
    return sigmoid * (1.0 + values * (1.0 - sigmoid))


def put_block(values, update, sample, depth_start):
    return lax.dynamic_update_slice(values, update, (0, sample, depth_start, 0))


def gather_taps(section, row_width):
    depth_len = section.shape[2] - 2
    plane_size = section.shape[3]
    flattened = jnp.pad(section, ((0, 0), (0, 0), (0, 0), (row_width + 1, row_width + 1)))
    column = lax.broadcasted_iota(jnp.int32, (1, 1, 1, plane_size), 3) % row_width
    left_mask = (column >= 1).astype(section.dtype)
    right_mask = (column <= row_width - 2).astype(section.dtype)
    pieces = []
    for tap_index in range(27):
        depth_start = tap_index // 9
        row_step = tap_index // 3 % 3 - 1
        col_step = tap_index % 3 - 1
        offset = row_width + 1 + row_step * row_width + col_step
        shifted = flattened[
            :, :, depth_start : depth_start + depth_len, offset : offset + plane_size
        ]
        if col_step < 0:
            shifted = shifted * left_mask
        elif col_step > 0:
            shifted = shifted * right_mask
        pieces.append(shifted)
    return jnp.concatenate(pieces, axis=0)


def apply_weight(patches, weight):
    flat_weight = weight.reshape(weight.shape[0] * weight.shape[1], weight.shape[2])
    return jnp.einsum("ko,kgzp->ogzp", flat_weight, patches, preferred_element_type=jnp.float32)


def weight_term(patches, grad_block, in_channels):
    summed = jnp.einsum("kgzp,ogzp->ko", patches, grad_block, preferred_element_type=jnp.float32)
    return summed.reshape(27, in_channels, grad_block.shape[0])


def pool_cells(values, row_width):
    channels, samples, depth_len, plane_size = values.shape
    row_count = plane_size // row_width
    grouped = values.reshape(
        channels, samples, depth_len // 2, 2, row_count // 2, 2, row_width // 2, 2
    )
    return grouped.mean(axis=(3, 5, 7)).reshape(channels, samples, depth_len // 2, plane_size // 4)


def spread_cells(values, coarse_width):
    channels, samples, depth_len, plane_size = values.shape
    row_count = plane_size // coarse_width
    grouped = values.reshape(channels, samples, depth_len, 1, row_count, 1, coarse_width, 1)
    grouped = jnp.broadcast_to(
        grouped, (channels, samples, depth_len, 2, row_count, 2, coarse_width, 2)
    )
    return grouped.reshape(channels, samples, 2 * depth_len, 4 * plane_size) * 0.125


def forward_layer(padded, weight, bias_values, row_width, depth_block, pooled_out):
    out_channels = weight.shape[2]
    samples, depth_total, plane_size = (padded.shape[1], padded.shape[2] - 2, padded.shape[3])
    per_sample = depth_total // depth_block
    pre_buffer = jnp.zeros((out_channels, samples, depth_total, plane_size), jnp.bfloat16)
    if pooled_out:
        out_buffer = jnp.zeros(
            (out_channels, samples, depth_total // 2, plane_size // 4), jnp.bfloat16
        )
    else:
        out_buffer = jnp.zeros_like(pre_buffer)

    def forward_block_step(block_index, buffers):
        sample = block_index // per_sample
        depth_start = block_index % per_sample * depth_block
        pre_values = (
            apply_weight(gather_taps(padded, row_width), weight) + bias_values[:, None, None, None]
        ).astype(jnp.bfloat16)
        activated = jax.nn.silu(pre_values.astype(jnp.float32))
        if pooled_out:
            result = put_block(
                buffers[1],
                pool_cells(activated, row_width).astype(jnp.bfloat16),
                sample,
                depth_start // 2,
            )
        else:
            result = put_block(buffers[1], activated.astype(jnp.bfloat16), sample, depth_start)
        return (put_block(buffers[0], pre_values, sample, depth_start), result)

    return lax.fori_loop(0, samples * per_sample, forward_block_step, (pre_buffer, out_buffer))


def weight_grads(padded, delta_values, row_width, depth_block, weight):
    samples, depth_total = (delta_values.shape[1], delta_values.shape[2])
    per_sample = depth_total // depth_block
    in_channels = weight.shape[1]

    def weight_block_step(block_index, summed):
        return summed + weight_term(gather_taps(padded, row_width), delta_values, in_channels)

    return lax.fori_loop(
        0, samples * per_sample, weight_block_step, jnp.zeros(weight.shape, jnp.float32)
    )


def data_grads(padded, flipped, row_width, depth_block):
    out_channels = flipped.shape[2]
    samples, depth_total, plane_size = (padded.shape[1], padded.shape[2] - 2, padded.shape[3])
    per_sample = depth_total // depth_block
    out_buffer = jnp.zeros((out_channels, samples, depth_total, plane_size), jnp.bfloat16)

    def data_block_step(block_index, buffer_now):
        sample = block_index // per_sample
        depth_start = block_index % per_sample * depth_block
        result = apply_weight(gather_taps(padded, row_width), flipped).astype(jnp.bfloat16)
        return put_block(buffer_now, result, sample, depth_start)

    return lax.fori_loop(0, samples * per_sample, data_block_step, out_buffer)


def parity_pool(values):
    c, n, z, parities, size = values.shape
    return values.reshape(c, n, z // 2, 2 * parities, size).mean(axis=3)

def parity_spread(values):
    c, n, z, size = values.shape
    grouped = jnp.broadcast_to(values[:, :, :, None, None, :], (c, n, z, 2, 4, size))
    return grouped.reshape(c, n, 2 * z, 4, size) * 0.125


def parity_permutation(row_width, chunk=128):
    lane = jnp.arange(chunk)
    yy, x = lane // row_width, lane % row_width
    target = ((yy % 2) * 2 + x % 2) * (chunk // 4) + (yy // 2) * (row_width // 2) + x // 2
    return (target[:, None] == jnp.arange(chunk)[None, :]).astype(jnp.bfloat16)

def _parity_kernel(coarse_width, channels, src_ref, perm_ref, w_ref, b_ref, out_ref, shifted_ref, sub_ref):
    rows_total, plane = src_ref.shape
    depth = rows_total // channels
    chunk = perm_ref.shape[0]
    quarter = chunk // 4
    for g in range(plane // chunk):
        moved = jnp.dot(src_ref[:, g * chunk : (g + 1) * chunk], perm_ref[...], preferred_element_type=jnp.float32)
        for s in range(4):
            sub_ref[s, :, g * quarter : (g + 1) * quarter] = moved[:, s * quarter : (s + 1) * quarter]
    size = plane // 4
    lane = lax.broadcasted_iota(jnp.int32, (channels, size), 1)
    row = lane // coarse_width
    col = lane % coarse_width
    rows = size // coarse_width
    for source_plane in range(depth):
        cache = {}
        for a in range(2):
            for b in range(2):
                for shift_index in range(9):
                    row_sum = a + shift_index // 3 - 1
                    col_sum = b + shift_index % 3 - 1
                    key = (row_sum % 2, col_sum % 2, row_sum // 2, col_sum // 2)
                    if key not in cache:
                        source, row_step, col_step = key[0] * 2 + key[1], key[2], key[3]
                        values = sub_ref[source, source_plane * channels : (source_plane + 1) * channels, :]
                        step = row_step * coarse_width + col_step
                        if step != 0:
                            values = pltpu.roll(values, (-step) % size, 1)
                        valid = (
                            (row + row_step >= 0) & (row + row_step < rows)
                            & (col + col_step >= 0) & (col + col_step < coarse_width)
                        )
                        cache[key] = jnp.where(valid, values, 0.0).astype(shifted_ref.dtype)
                    shifted_ref[source_plane, a * 2 + b, shift_index * channels : (shift_index + 1) * channels, :] = cache[key]
    for z in range(out_ref.shape[1]):
        for parity in range(4):
            summed = b_ref[...] + jnp.zeros((out_ref.shape[0], size), jnp.float32)
            for dz in range(3):
                summed = summed + jnp.dot(
                    w_ref[dz], shifted_ref[z + dz, parity], preferred_element_type=jnp.float32
                )
            out_ref[:, z, parity, :] = summed.astype(out_ref.dtype)

def parity_conv_forward(padded, weight, bias_values, row_width):
    channels, depth, plane = padded.shape
    out_channels = weight.shape[2]
    per_depth = weight.reshape(3, 9 * channels, out_channels).transpose(0, 2, 1)
    by_plane = padded.transpose(1, 0, 2).reshape(depth * channels, plane)
    return pl.pallas_call(
        functools.partial(_parity_kernel, row_width // 2, channels),
        out_shape=(
            jax.ShapeDtypeStruct((out_channels, depth - 2, 4, plane // 4), jnp.bfloat16),
            jax.ShapeDtypeStruct((depth, 4, 9 * channels, plane // 4), jnp.bfloat16),
        ),
        scratch_shapes=[pltpu.VMEM((4, depth * channels, plane // 4), jnp.float32)],
    )(by_plane, parity_permutation(row_width), per_depth, bias_values.reshape(out_channels, 1))


def parity_weight_grad(shifted, delta):
    depth_len = delta.shape[1]
    per_depth = [
        jnp.einsum(
            "zpkq,ozpq->ko", shifted[dz : dz + depth_len], delta, preferred_element_type=jnp.float32
        )
        for dz in range(3)
    ]
    return jnp.stack(per_depth).reshape(27, shifted.shape[2] // 9, delta.shape[0])


def bias_sum(delta_values):
    return jnp.sum(delta_values, axis=(1, 2, 3), dtype=jnp.float32)


def per_device(volume, cotangent, w_first, b_first, w_second, b_second, w_third, b_third):
    flipped_second = jnp.flip(w_second, 0).transpose(0, 2, 1)
    flipped_third = jnp.flip(w_third, 0).transpose(0, 2, 1)
    volume_padded = with_halo(volume, (("slab", 2),), 1)
    first_layer = [
        parity_conv_forward(volume_padded[:, s], w_first, b_first, SX)
        for s in range(volume_padded.shape[1])
    ]
    first_pre = jnp.stack([pre for pre, _ in first_layer], axis=1)
    first_pooled = parity_pool(jax.nn.silu(first_pre.astype(jnp.float32))).astype(jnp.bfloat16)
    first_padded = with_halo(first_pooled, (("slab", 2),), 1)
    second_pre, second_pooled = forward_layer(
        first_padded, w_second, b_second, SX // 2, CZ // 2, True
    )
    coarse_depth = second_pooled.shape[2]
    third_padded = with_halo(second_pooled, (("slab", 2),), 1)
    third_pre, features = forward_layer(
        third_padded, w_third, b_third, SX // 4, coarse_depth, False
    )
    third_delta = (
        cotangent.astype(jnp.float32) * silu_slope(third_pre.astype(jnp.float32))
    ).astype(jnp.bfloat16)
    kernel_third = weight_grads(third_padded, third_delta, SX // 4, coarse_depth, w_third)
    bias_third = bias_sum(third_delta)
    kernel_third, bias_third = all_reduce_rows((kernel_third, bias_third))
    delta_window = with_halo(third_delta, (("slab", 2),), 1)
    second_back = data_grads(delta_window, flipped_third, SX // 4, coarse_depth)
    second_delta = (
        spread_cells(second_back.astype(jnp.float32), SX // 4)
        * silu_slope(second_pre.astype(jnp.float32))
    ).astype(jnp.bfloat16)
    kernel_second = weight_grads(first_padded, second_delta, SX // 2, CZ // 2, w_second)
    bias_second = bias_sum(second_delta)
    delta_padded = with_halo(second_delta, (("slab", 2),), 1)
    first_back = data_grads(delta_padded, flipped_second, SX // 2, CZ // 2)
    first_delta = (
        parity_spread(first_back.astype(jnp.float32)) * silu_slope(first_pre.astype(jnp.float32))
    ).astype(jnp.bfloat16)
    kernel_first = sum(
        parity_weight_grad(shifted, first_delta[:, s])
        for s, (_, shifted) in enumerate(first_layer)
    )
    bias_first = jnp.sum(first_delta, axis=(1, 2, 3, 4), dtype=jnp.float32)
    kernel_second, kernel_first, bias_second, bias_first = all_reduce_rows(
        (kernel_second, kernel_first, bias_second, bias_first)
    )
    return (
        features,
        kernel_first,
        bias_first,
        kernel_second,
        bias_second,
        kernel_third,
        bias_third,
    )


def xor_pairs(axis, mask):
    return [(i, i ^ mask) for i in range(lax.axis_size(axis))]


def all_reduce_rows(grads, halving_steps=3, lanes=128):
    steps = []
    for axis in ("sample", "slab"):
        mask = 1
        while mask < lax.axis_size(axis):
            steps.append((axis, mask))
            mask *= 2
    pieces, offsets = [], []
    rows = 0
    for g in grads:
        count = -(-g.size // lanes)
        flat = g.reshape(-1)
        flat = jnp.pad(flat, (0, count * lanes - g.size))
        pieces.append(flat.reshape(count, lanes))
        offsets.append(rows)
        rows += count
    block = 8 << halving_steps
    total = -(-rows // block) * block
    if total > rows:
        pieces.append(jnp.zeros((total - rows, lanes), jnp.float32))
    buffer = jnp.concatenate(pieces, axis=0)
    kept = []
    for axis, mask in steps[:halving_steps]:
        half = buffer.shape[0] // 2
        upper = ((lax.axis_index(axis) // mask) % 2).astype(jnp.int32)
        send = lax.dynamic_slice_in_dim(buffer, (1 - upper) * half, half, axis=0)
        keep = lax.dynamic_slice_in_dim(buffer, upper * half, half, axis=0)
        buffer = keep + lax.ppermute(send, axis, xor_pairs(axis, mask))
        kept.append((axis, mask, upper))
    for axis, mask in steps[halving_steps:]:
        buffer = buffer + lax.ppermute(buffer, axis, xor_pairs(axis, mask))
    for axis, mask, upper in reversed(kept):
        other = lax.ppermute(buffer, axis, xor_pairs(axis, mask))
        pair = jnp.stack([buffer, other])
        first = lax.dynamic_index_in_dim(pair, upper, axis=0, keepdims=False)
        second = lax.dynamic_index_in_dim(pair, 1 - upper, axis=0, keepdims=False)
        buffer = jnp.concatenate([first, second], axis=0)
    out = []
    for g, start in zip(grads, offsets):
        count = -(-g.size // lanes)
        part = buffer[start : start + count].reshape(-1)[: g.size]
        out.append(part.reshape(g.shape))
    return tuple(out)


def solution(mesh):
    in_specs = (
        P(None, "sample", "slab", None),
        P(None, "sample", "slab", None),
        P(),
        P(),
        P(),
        P(),
        P(),
        P(),
    )
    out_specs = (P(None, "sample", "slab", None), P(), P(), P(), P(), P(), P())
    return jax.shard_map(
        per_device, mesh=mesh, in_specs=in_specs, out_specs=out_specs, check_vma=False
    )
```

```python
import functools

import jax
import jax.numpy as jnp
from jax import lax
from jax.experimental import pallas as pl
from jax.experimental.pallas import tpu as pltpu
from jax.sharding import PartitionSpec as P

SX = 32
CZ = 4


def with_halo(shard, sides, width):
    for axis, dim in sides:
        size, length = (lax.axis_size(axis), shard.shape[dim])
        up = [(i, (i + 1) % size) for i in range(size - 1)]
        down = [(j, i) for i, j in up]
        last = lax.slice_in_dim(shard, length - width, length, axis=dim)
        first = lax.slice_in_dim(shard, 0, width, axis=dim)
        before = lax.ppermute(last, axis, up)
        after = lax.ppermute(first, axis, down)
        shard = jnp.concatenate([before, shard, after], axis=dim)
    return shard


def silu_slope(values):
    sigmoid = jax.nn.sigmoid(values)
    return sigmoid * (1.0 + values * (1.0 - sigmoid))


def put_block(values, update, sample, depth_start):
    return lax.dynamic_update_slice(values, update, (0, sample, depth_start, 0))


def gather_taps(section, row_width):
    depth_len = section.shape[2] - 2
    plane_size = section.shape[3]
    flattened = jnp.pad(section, ((0, 0), (0, 0), (0, 0), (row_width + 1, row_width + 1)))
    column = lax.broadcasted_iota(jnp.int32, (1, 1, 1, plane_size), 3) % row_width
    left_mask = (column >= 1).astype(section.dtype)
    right_mask = (column <= row_width - 2).astype(section.dtype)
    pieces = []
    for tap_index in range(27):
        depth_start = tap_index // 9
        row_step = tap_index // 3 % 3 - 1
        col_step = tap_index % 3 - 1
        offset = row_width + 1 + row_step * row_width + col_step
        shifted = flattened[
            :, :, depth_start : depth_start + depth_len, offset : offset + plane_size
        ]
        if col_step < 0:
            shifted = shifted * left_mask
        elif col_step > 0:
            shifted = shifted * right_mask
        pieces.append(shifted)
    return jnp.concatenate(pieces, axis=0)


def apply_weight(patches, weight):
    flat_weight = weight.reshape(weight.shape[0] * weight.shape[1], weight.shape[2])
    return jnp.einsum("ko,kgzp->ogzp", flat_weight, patches, preferred_element_type=jnp.float32)


def weight_term(patches, grad_block, in_channels):
    summed = jnp.einsum("kgzp,ogzp->ko", patches, grad_block, preferred_element_type=jnp.float32)
    return summed.reshape(27, in_channels, grad_block.shape[0])


def pool_cells(values, row_width):
    channels, samples, depth_len, plane_size = values.shape
    row_count = plane_size // row_width
    grouped = values.reshape(
        channels, samples, depth_len // 2, 2, row_count // 2, 2, row_width // 2, 2
    )
    return grouped.mean(axis=(3, 5, 7)).reshape(channels, samples, depth_len // 2, plane_size // 4)


def spread_cells(values, coarse_width):
    channels, samples, depth_len, plane_size = values.shape
    row_count = plane_size // coarse_width
    grouped = values.reshape(channels, samples, depth_len, 1, row_count, 1, coarse_width, 1)
    grouped = jnp.broadcast_to(
        grouped, (channels, samples, depth_len, 2, row_count, 2, coarse_width, 2)
    )
    return grouped.reshape(channels, samples, 2 * depth_len, 4 * plane_size) * 0.125


def forward_layer(padded, weight, bias_values, row_width, depth_block, pooled_out):
    out_channels = weight.shape[2]
    samples, depth_total, plane_size = (padded.shape[1], padded.shape[2] - 2, padded.shape[3])
    per_sample = depth_total // depth_block
    pre_buffer = jnp.zeros((out_channels, samples, depth_total, plane_size), jnp.bfloat16)
    if pooled_out:
        out_buffer = jnp.zeros(
            (out_channels, samples, depth_total // 2, plane_size // 4), jnp.bfloat16
        )
    else:
        out_buffer = jnp.zeros_like(pre_buffer)

    def forward_block_step(block_index, buffers):
        sample = block_index // per_sample
        depth_start = block_index % per_sample * depth_block
        pre_values = (
            apply_weight(gather_taps(padded, row_width), weight) + bias_values[:, None, None, None]
        ).astype(jnp.bfloat16)
        activated = jax.nn.silu(pre_values.astype(jnp.float32))
        if pooled_out:
            result = put_block(
                buffers[1],
                pool_cells(activated, row_width).astype(jnp.bfloat16),
                sample,
                depth_start // 2,
            )
        else:
            result = put_block(buffers[1], activated.astype(jnp.bfloat16), sample, depth_start)
        return (put_block(buffers[0], pre_values, sample, depth_start), result)

    return lax.fori_loop(0, samples * per_sample, forward_block_step, (pre_buffer, out_buffer))


def weight_grads(padded, delta_values, row_width, depth_block, weight):
    samples, depth_total = (delta_values.shape[1], delta_values.shape[2])
    per_sample = depth_total // depth_block
    in_channels = weight.shape[1]

    def weight_block_step(block_index, summed):
        return summed + weight_term(gather_taps(padded, row_width), delta_values, in_channels)

    return lax.fori_loop(
        0, samples * per_sample, weight_block_step, jnp.zeros(weight.shape, jnp.float32)
    )


def data_grads(padded, flipped, row_width, depth_block):
    out_channels = flipped.shape[2]
    samples, depth_total, plane_size = (padded.shape[1], padded.shape[2] - 2, padded.shape[3])
    per_sample = depth_total // depth_block
    out_buffer = jnp.zeros((out_channels, samples, depth_total, plane_size), jnp.bfloat16)

    def data_block_step(block_index, buffer_now):
        sample = block_index // per_sample
        depth_start = block_index % per_sample * depth_block
        result = apply_weight(gather_taps(padded, row_width), flipped).astype(jnp.bfloat16)
        return put_block(buffer_now, result, sample, depth_start)

    return lax.fori_loop(0, samples * per_sample, data_block_step, out_buffer)


def parity_pool(values):
    c, n, z, parities, size = values.shape
    return values.reshape(c, n, z // 2, 2 * parities, size).mean(axis=3)

def parity_spread(values):
    c, n, z, size = values.shape
    grouped = jnp.broadcast_to(values[:, :, :, None, None, :], (c, n, z, 2, 4, size))
    return grouped.reshape(c, n, 2 * z, 4, size) * 0.125


def parity_permutation(row_width, chunk=128):
    lane = jnp.arange(chunk)
    yy, x = lane // row_width, lane % row_width
    target = ((yy % 2) * 2 + x % 2) * (chunk // 4) + (yy // 2) * (row_width // 2) + x // 2
    return (target[:, None] == jnp.arange(chunk)[None, :]).astype(jnp.bfloat16)

def _parity_kernel(coarse_width, channels, src_ref, perm_ref, w_ref, b_ref, out_ref, shifted_ref, sub_ref):
    rows_total, plane = src_ref.shape
    depth = rows_total // channels
    chunk = perm_ref.shape[0]
    quarter = chunk // 4
    for g in range(plane // chunk):
        moved = jnp.dot(src_ref[:, g * chunk : (g + 1) * chunk], perm_ref[...], preferred_element_type=jnp.float32)
        for s in range(4):
            sub_ref[s, :, g * quarter : (g + 1) * quarter] = moved[:, s * quarter : (s + 1) * quarter]
    size = plane // 4
    lane = lax.broadcasted_iota(jnp.int32, (channels, size), 1)
    row = lane // coarse_width
    col = lane % coarse_width
    rows = size // coarse_width
    for source_plane in range(depth):
        cache = {}
        for a in range(2):
            for b in range(2):
                for shift_index in range(9):
                    row_sum = a + shift_index // 3 - 1
                    col_sum = b + shift_index % 3 - 1
                    key = (row_sum % 2, col_sum % 2, row_sum // 2, col_sum // 2)
                    if key not in cache:
                        source, row_step, col_step = key[0] * 2 + key[1], key[2], key[3]
                        values = sub_ref[source, source_plane * channels : (source_plane + 1) * channels, :]
                        step = row_step * coarse_width + col_step
                        if step != 0:
                            values = pltpu.roll(values, (-step) % size, 1)
                        valid = (
                            (row + row_step >= 0) & (row + row_step < rows)
                            & (col + col_step >= 0) & (col + col_step < coarse_width)
                        )
                        cache[key] = jnp.where(valid, values, 0.0).astype(shifted_ref.dtype)
                    shifted_ref[source_plane, a * 2 + b, shift_index * channels : (shift_index + 1) * channels, :] = cache[key]
    for z in range(out_ref.shape[1]):
        for parity in range(4):
            summed = b_ref[...] + jnp.zeros((out_ref.shape[0], size), jnp.float32)
            for dz in range(3):
                summed = summed + jnp.dot(
                    w_ref[dz], shifted_ref[z + dz, parity], preferred_element_type=jnp.float32
                )
            out_ref[:, z, parity, :] = summed.astype(out_ref.dtype)

def parity_conv_forward(padded, weight, bias_values, row_width):
    channels, depth, plane = padded.shape
    out_channels = weight.shape[2]
    per_depth = weight.reshape(3, 9 * channels, out_channels).transpose(0, 2, 1)
    by_plane = padded.transpose(1, 0, 2).reshape(depth * channels, plane)
    return pl.pallas_call(
        functools.partial(_parity_kernel, row_width // 2, channels),
        out_shape=(
            jax.ShapeDtypeStruct((out_channels, depth - 2, 4, plane // 4), jnp.bfloat16),
            jax.ShapeDtypeStruct((depth, 4, 9 * channels, plane // 4), jnp.bfloat16),
        ),
        scratch_shapes=[pltpu.VMEM((4, depth * channels, plane // 4), jnp.float32)],
    )(by_plane, parity_permutation(row_width), per_depth, bias_values.reshape(out_channels, 1))


def parity_weight_grad(shifted, delta):
    depth_len = delta.shape[1]
    per_depth = [
        jnp.einsum(
            "zpkq,ozpq->ko", shifted[dz : dz + depth_len], delta, preferred_element_type=jnp.float32
        )
        for dz in range(3)
    ]
    return jnp.stack(per_depth).reshape(27, shifted.shape[2] // 9, delta.shape[0])


def bias_sum(delta_values):
    return jnp.sum(delta_values, axis=(1, 2, 3), dtype=jnp.float32)


def per_device(volume, cotangent, w_first, b_first, w_second, b_second, w_third, b_third):
    flipped_second = jnp.flip(w_second, 0).transpose(0, 2, 1)
    flipped_third = jnp.flip(w_third, 0).transpose(0, 2, 1)
    volume_padded = with_halo(volume, (("slab", 2),), 1)
    first_layer = [
        parity_conv_forward(volume_padded[:, s], w_first, b_first, SX)
        for s in range(volume_padded.shape[1])
    ]
    first_pre = jnp.stack([pre for pre, _ in first_layer], axis=1)
    first_pooled = parity_pool(jax.nn.silu(first_pre.astype(jnp.float32))).astype(jnp.bfloat16)
    first_padded = with_halo(first_pooled, (("slab", 2),), 1)
    second_pre, second_pooled = forward_layer(
        first_padded, w_second, b_second, SX // 2, CZ // 2, True
    )
    coarse_depth = second_pooled.shape[2]
    third_padded = with_halo(second_pooled, (("slab", 2),), 1)
    third_pre, features = forward_layer(
        third_padded, w_third, b_third, SX // 4, coarse_depth, False
    )
    third_delta = (
        cotangent.astype(jnp.float32) * silu_slope(third_pre.astype(jnp.float32))
    ).astype(jnp.bfloat16)
    kernel_third = weight_grads(third_padded, third_delta, SX // 4, coarse_depth, w_third)
    bias_third = bias_sum(third_delta)
    delta_window = with_halo(third_delta, (("slab", 2),), 1)
    second_back = data_grads(delta_window, flipped_third, SX // 4, coarse_depth)
    second_delta = (
        spread_cells(second_back.astype(jnp.float32), SX // 4)
        * silu_slope(second_pre.astype(jnp.float32))
    ).astype(jnp.bfloat16)
    kernel_second = weight_grads(first_padded, second_delta, SX // 2, CZ // 2, w_second)
    bias_second = bias_sum(second_delta)
    delta_padded = with_halo(second_delta, (("slab", 2),), 1)
    first_back = data_grads(delta_padded, flipped_second, SX // 2, CZ // 2)
    first_delta = (
        parity_spread(first_back.astype(jnp.float32)) * silu_slope(first_pre.astype(jnp.float32))
    ).astype(jnp.bfloat16)
    kernel_first = sum(
        parity_weight_grad(shifted, first_delta[:, s])
        for s, (_, shifted) in enumerate(first_layer)
    )
    bias_first = jnp.sum(first_delta, axis=(1, 2, 3, 4), dtype=jnp.float32)
    weights = all_reduce_rows(
        (kernel_third, kernel_second, kernel_first, bias_third, bias_second, bias_first)
    )
    kernel_third, kernel_second, kernel_first, bias_third, bias_second, bias_first = weights
    return (
        features,
        kernel_first,
        bias_first,
        kernel_second,
        bias_second,
        kernel_third,
        bias_third,
    )


def xor_pairs(axis, mask):
    return [(i, i ^ mask) for i in range(lax.axis_size(axis))]


def all_reduce_rows(grads, halving_steps=5, lanes=128):
    steps = []
    for axis in ("sample", "slab"):
        mask = 1
        while mask < lax.axis_size(axis):
            steps.append((axis, mask))
            mask *= 2
    pieces, offsets = [], []
    rows = 0
    for g in grads:
        count = -(-g.size // lanes)
        flat = g.reshape(-1)
        flat = jnp.pad(flat, (0, count * lanes - g.size))
        pieces.append(flat.reshape(count, lanes))
        offsets.append(rows)
        rows += count
    block = 8 << halving_steps
    total = -(-rows // block) * block
    if total > rows:
        pieces.append(jnp.zeros((total - rows, lanes), jnp.float32))
    buffer = jnp.concatenate(pieces, axis=0)
    kept = []
    for axis, mask in steps[:halving_steps]:
        half = buffer.shape[0] // 2
        upper = ((lax.axis_index(axis) // mask) % 2).astype(jnp.int32)
        send = lax.dynamic_slice_in_dim(buffer, (1 - upper) * half, half, axis=0)
        keep = lax.dynamic_slice_in_dim(buffer, upper * half, half, axis=0)
        buffer = keep + lax.ppermute(send, axis, xor_pairs(axis, mask))
        kept.append((axis, mask, upper))
    for axis, mask in steps[halving_steps:]:
        buffer = buffer + lax.ppermute(buffer, axis, xor_pairs(axis, mask))
    for axis, mask, upper in reversed(kept):
        other = lax.ppermute(buffer, axis, xor_pairs(axis, mask))
        pair = jnp.stack([buffer, other])
        first = lax.dynamic_index_in_dim(pair, upper, axis=0, keepdims=False)
        second = lax.dynamic_index_in_dim(pair, 1 - upper, axis=0, keepdims=False)
        buffer = jnp.concatenate([first, second], axis=0)
    out = []
    for g, start in zip(grads, offsets):
        count = -(-g.size // lanes)
        part = buffer[start : start + count].reshape(-1)[: g.size]
        out.append(part.reshape(g.shape))
    return tuple(out)


def solution(mesh):
    in_specs = (
        P(None, "sample", "slab", None),
        P(None, "sample", "slab", None),
        P(),
        P(),
        P(),
        P(),
        P(),
        P(),
    )
    out_specs = (P(None, "sample", "slab", None), P(), P(), P(), P(), P(), P())
    return jax.shard_map(
        per_device, mesh=mesh, in_specs=in_specs, out_specs=out_specs, check_vma=False
    )
```

```python
import functools

import jax
import jax.numpy as jnp
from jax import lax
from jax.experimental import pallas as pl
from jax.experimental.pallas import tpu as pltpu
from jax.sharding import PartitionSpec as P

SX = 32
CZ = 4


def with_halo(shard, sides, width):
    for axis, dim in sides:
        size, length = (lax.axis_size(axis), shard.shape[dim])
        up = [(i, (i + 1) % size) for i in range(size - 1)]
        down = [(j, i) for i, j in up]
        last = lax.slice_in_dim(shard, length - width, length, axis=dim)
        first = lax.slice_in_dim(shard, 0, width, axis=dim)
        before = lax.ppermute(last, axis, up)
        after = lax.ppermute(first, axis, down)
        shard = jnp.concatenate([before, shard, after], axis=dim)
    return shard


def silu_slope(values):
    sigmoid = jax.nn.sigmoid(values)
    return sigmoid * (1.0 + values * (1.0 - sigmoid))


def put_block(values, update, sample, depth_start):
    return lax.dynamic_update_slice(values, update, (0, sample, depth_start, 0))


def gather_taps(section, row_width):
    depth_len = section.shape[2] - 2
    plane_size = section.shape[3]
    flattened = jnp.pad(section, ((0, 0), (0, 0), (0, 0), (row_width + 1, row_width + 1)))
    column = lax.broadcasted_iota(jnp.int32, (1, 1, 1, plane_size), 3) % row_width
    left_mask = (column >= 1).astype(section.dtype)
    right_mask = (column <= row_width - 2).astype(section.dtype)
    pieces = []
    for tap_index in range(27):
        depth_start = tap_index // 9
        row_step = tap_index // 3 % 3 - 1
        col_step = tap_index % 3 - 1
        offset = row_width + 1 + row_step * row_width + col_step
        shifted = flattened[
            :, :, depth_start : depth_start + depth_len, offset : offset + plane_size
        ]
        if col_step < 0:
            shifted = shifted * left_mask
        elif col_step > 0:
            shifted = shifted * right_mask
        pieces.append(shifted)
    return jnp.concatenate(pieces, axis=0)


def apply_weight(patches, weight):
    flat_weight = weight.reshape(weight.shape[0] * weight.shape[1], weight.shape[2])
    return jnp.einsum("ko,kgzp->ogzp", flat_weight, patches, preferred_element_type=jnp.float32)


def weight_term(patches, grad_block, in_channels):
    summed = jnp.einsum("kgzp,ogzp->ko", patches, grad_block, preferred_element_type=jnp.float32)
    return summed.reshape(27, in_channels, grad_block.shape[0])


def pool_cells(values, row_width):
    channels, samples, depth_len, plane_size = values.shape
    row_count = plane_size // row_width
    grouped = values.reshape(
        channels, samples, depth_len // 2, 2, row_count // 2, 2, row_width // 2, 2
    )
    return grouped.mean(axis=(3, 5, 7)).reshape(channels, samples, depth_len // 2, plane_size // 4)


def spread_cells(values, coarse_width):
    channels, samples, depth_len, plane_size = values.shape
    row_count = plane_size // coarse_width
    grouped = values.reshape(channels, samples, depth_len, 1, row_count, 1, coarse_width, 1)
    grouped = jnp.broadcast_to(
        grouped, (channels, samples, depth_len, 2, row_count, 2, coarse_width, 2)
    )
    return grouped.reshape(channels, samples, 2 * depth_len, 4 * plane_size) * 0.125


def forward_layer(padded, weight, bias_values, row_width, depth_block, pooled_out):
    out_channels = weight.shape[2]
    samples, depth_total, plane_size = (padded.shape[1], padded.shape[2] - 2, padded.shape[3])
    per_sample = depth_total // depth_block
    pre_buffer = jnp.zeros((out_channels, samples, depth_total, plane_size), jnp.bfloat16)
    if pooled_out:
        out_buffer = jnp.zeros(
            (out_channels, samples, depth_total // 2, plane_size // 4), jnp.bfloat16
        )
    else:
        out_buffer = jnp.zeros_like(pre_buffer)

    def forward_block_step(block_index, buffers):
        sample = block_index // per_sample
        depth_start = block_index % per_sample * depth_block
        pre_values = (
            apply_weight(gather_taps(padded, row_width), weight) + bias_values[:, None, None, None]
        ).astype(jnp.bfloat16)
        activated = jax.nn.silu(pre_values.astype(jnp.float32))
        if pooled_out:
            result = put_block(
                buffers[1],
                pool_cells(activated, row_width).astype(jnp.bfloat16),
                sample,
                depth_start // 2,
            )
        else:
            result = put_block(buffers[1], activated.astype(jnp.bfloat16), sample, depth_start)
        return (put_block(buffers[0], pre_values, sample, depth_start), result)

    return lax.fori_loop(0, samples * per_sample, forward_block_step, (pre_buffer, out_buffer))


def weight_grads(padded, delta_values, row_width, depth_block, weight):
    samples, depth_total = (delta_values.shape[1], delta_values.shape[2])
    per_sample = depth_total // depth_block
    in_channels = weight.shape[1]

    def weight_block_step(block_index, summed):
        return summed + weight_term(gather_taps(padded, row_width), delta_values, in_channels)

    return lax.fori_loop(
        0, samples * per_sample, weight_block_step, jnp.zeros(weight.shape, jnp.float32)
    )


def data_grads(padded, flipped, row_width, depth_block):
    out_channels = flipped.shape[2]
    samples, depth_total, plane_size = (padded.shape[1], padded.shape[2] - 2, padded.shape[3])
    per_sample = depth_total // depth_block
    out_buffer = jnp.zeros((out_channels, samples, depth_total, plane_size), jnp.bfloat16)

    def data_block_step(block_index, buffer_now):
        sample = block_index // per_sample
        depth_start = block_index % per_sample * depth_block
        result = apply_weight(gather_taps(padded, row_width), flipped).astype(jnp.bfloat16)
        return put_block(buffer_now, result, sample, depth_start)

    return lax.fori_loop(0, samples * per_sample, data_block_step, out_buffer)


def parity_pool(values):
    c, n, z, parities, size = values.shape
    return values.reshape(c, n, z // 2, 2 * parities, size).mean(axis=3)

def parity_spread(values):
    c, n, z, size = values.shape
    grouped = jnp.broadcast_to(values[:, :, :, None, None, :], (c, n, z, 2, 4, size))
    return grouped.reshape(c, n, 2 * z, 4, size) * 0.125


def parity_permutation(row_width, chunk=128):
    lane = jnp.arange(chunk)
    yy, x = lane // row_width, lane % row_width
    target = ((yy % 2) * 2 + x % 2) * (chunk // 4) + (yy // 2) * (row_width // 2) + x // 2
    return (target[:, None] == jnp.arange(chunk)[None, :]).astype(jnp.bfloat16)

def _parity_kernel(coarse_width, channels, src_ref, perm_ref, w_ref, b_ref, out_ref, shifted_ref, sub_ref):
    rows_total, plane = src_ref.shape
    depth = rows_total // channels
    chunk = perm_ref.shape[0]
    quarter = chunk // 4
    for g in range(plane // chunk):
        moved = jnp.dot(src_ref[:, g * chunk : (g + 1) * chunk], perm_ref[...], preferred_element_type=jnp.float32)
        for s in range(4):
            sub_ref[s, :, g * quarter : (g + 1) * quarter] = moved[:, s * quarter : (s + 1) * quarter]
    size = plane // 4
    lane = lax.broadcasted_iota(jnp.int32, (channels, size), 1)
    row = lane // coarse_width
    col = lane % coarse_width
    rows = size // coarse_width
    for source_plane in range(depth):
        cache = {}
        for a in range(2):
            for b in range(2):
                for shift_index in range(9):
                    row_sum = a + shift_index // 3 - 1
                    col_sum = b + shift_index % 3 - 1
                    key = (row_sum % 2, col_sum % 2, row_sum // 2, col_sum // 2)
                    if key not in cache:
                        source, row_step, col_step = key[0] * 2 + key[1], key[2], key[3]
                        values = sub_ref[source, source_plane * channels : (source_plane + 1) * channels, :]
                        step = row_step * coarse_width + col_step
                        if step != 0:
                            values = pltpu.roll(values, (-step) % size, 1)
                        valid = (
                            (row + row_step >= 0) & (row + row_step < rows)
                            & (col + col_step >= 0) & (col + col_step < coarse_width)
                        )
                        cache[key] = jnp.where(valid, values, 0.0).astype(shifted_ref.dtype)
                    shifted_ref[source_plane, a * 2 + b, shift_index * channels : (shift_index + 1) * channels, :] = cache[key]
    for z in range(out_ref.shape[1]):
        for parity in range(4):
            summed = b_ref[...] + jnp.zeros((out_ref.shape[0], size), jnp.float32)
            for dz in range(3):
                summed = summed + jnp.dot(
                    w_ref[dz], shifted_ref[z + dz, parity], preferred_element_type=jnp.float32
                )
            out_ref[:, z, parity, :] = summed.astype(out_ref.dtype)

def parity_conv_forward(padded, weight, bias_values, row_width):
    channels, depth, plane = padded.shape
    out_channels = weight.shape[2]
    per_depth = weight.reshape(3, 9 * channels, out_channels).transpose(0, 2, 1)
    by_plane = padded.transpose(1, 0, 2).reshape(depth * channels, plane)
    return pl.pallas_call(
        functools.partial(_parity_kernel, row_width // 2, channels),
        out_shape=(
            jax.ShapeDtypeStruct((out_channels, depth - 2, 4, plane // 4), jnp.bfloat16),
            jax.ShapeDtypeStruct((depth, 4, 9 * channels, plane // 4), jnp.bfloat16),
        ),
        scratch_shapes=[pltpu.VMEM((4, depth * channels, plane // 4), jnp.float32)],
    )(by_plane, parity_permutation(row_width), per_depth, bias_values.reshape(out_channels, 1))


def parity_weight_grad(shifted, delta):
    depth = shifted.shape[0]
    depth_len = delta.shape[1]
    placed = jnp.stack(
        [jnp.pad(delta, ((0, 0), (dz, depth - depth_len - dz), (0, 0), (0, 0))) for dz in range(3)]
    )
    summed = jnp.einsum("zpkq,dozpq->dko", shifted, placed, preferred_element_type=jnp.float32)
    return summed.reshape(27, shifted.shape[2] // 9, delta.shape[0])


def bias_sum(delta_values):
    return jnp.sum(delta_values, axis=(1, 2, 3), dtype=jnp.float32)


def per_device(volume, cotangent, w_first, b_first, w_second, b_second, w_third, b_third):
    flipped_second = jnp.flip(w_second, 0).transpose(0, 2, 1)
    flipped_third = jnp.flip(w_third, 0).transpose(0, 2, 1)
    volume_padded = with_halo(volume, (("slab", 2),), 1)
    first_layer = [
        parity_conv_forward(volume_padded[:, s], w_first, b_first, SX)
        for s in range(volume_padded.shape[1])
    ]
    first_pre = jnp.stack([pre for pre, _ in first_layer], axis=1)
    first_pooled = parity_pool(jax.nn.silu(first_pre.astype(jnp.float32))).astype(jnp.bfloat16)
    first_padded = with_halo(first_pooled, (("slab", 2),), 1)
    second_pre, second_pooled = forward_layer(
        first_padded, w_second, b_second, SX // 2, CZ // 2, True
    )
    coarse_depth = second_pooled.shape[2]
    third_padded = with_halo(second_pooled, (("slab", 2),), 1)
    third_pre, features = forward_layer(
        third_padded, w_third, b_third, SX // 4, coarse_depth, False
    )
    third_delta = (
        cotangent.astype(jnp.float32) * silu_slope(third_pre.astype(jnp.float32))
    ).astype(jnp.bfloat16)
    kernel_third = weight_grads(third_padded, third_delta, SX // 4, coarse_depth, w_third)
    bias_third = bias_sum(third_delta)
    delta_window = with_halo(third_delta, (("slab", 2),), 1)
    second_back = data_grads(delta_window, flipped_third, SX // 4, coarse_depth)
    second_delta = (
        spread_cells(second_back.astype(jnp.float32), SX // 4)
        * silu_slope(second_pre.astype(jnp.float32))
    ).astype(jnp.bfloat16)
    kernel_second = weight_grads(first_padded, second_delta, SX // 2, CZ // 2, w_second)
    bias_second = bias_sum(second_delta)
    delta_padded = with_halo(second_delta, (("slab", 2),), 1)
    first_back = data_grads(delta_padded, flipped_second, SX // 2, CZ // 2)
    first_delta = (
        parity_spread(first_back.astype(jnp.float32)) * silu_slope(first_pre.astype(jnp.float32))
    ).astype(jnp.bfloat16)
    kernel_first = sum(
        parity_weight_grad(shifted, first_delta[:, s])
        for s, (_, shifted) in enumerate(first_layer)
    )
    bias_first = jnp.sum(first_delta, axis=(1, 2, 3, 4), dtype=jnp.float32)
    weights = all_reduce_rows(
        (kernel_third, kernel_second, kernel_first, bias_third, bias_second, bias_first)
    )
    kernel_third, kernel_second, kernel_first, bias_third, bias_second, bias_first = weights
    return (
        features,
        kernel_first,
        bias_first,
        kernel_second,
        bias_second,
        kernel_third,
        bias_third,
    )


def xor_pairs(axis, mask):
    return [(i, i ^ mask) for i in range(lax.axis_size(axis))]


def all_reduce_rows(grads, halving_steps=5, lanes=128):
    steps = []
    for axis in ("sample", "slab"):
        mask = 1
        while mask < lax.axis_size(axis):
            steps.append((axis, mask))
            mask *= 2
    pieces, offsets = [], []
    rows = 0
    for g in grads:
        count = -(-g.size // lanes)
        flat = g.reshape(-1)
        flat = jnp.pad(flat, (0, count * lanes - g.size))
        pieces.append(flat.reshape(count, lanes))
        offsets.append(rows)
        rows += count
    block = 8 << halving_steps
    total = -(-rows // block) * block
    if total > rows:
        pieces.append(jnp.zeros((total - rows, lanes), jnp.float32))
    buffer = jnp.concatenate(pieces, axis=0)
    kept = []
    for axis, mask in steps[:halving_steps]:
        half = buffer.shape[0] // 2
        upper = ((lax.axis_index(axis) // mask) % 2).astype(jnp.int32)
        send = lax.dynamic_slice_in_dim(buffer, (1 - upper) * half, half, axis=0)
        keep = lax.dynamic_slice_in_dim(buffer, upper * half, half, axis=0)
        buffer = keep + lax.ppermute(send, axis, xor_pairs(axis, mask))
        kept.append((axis, mask, upper))
    for axis, mask in steps[halving_steps:]:
        buffer = buffer + lax.ppermute(buffer, axis, xor_pairs(axis, mask))
    for axis, mask, upper in reversed(kept):
        other = lax.ppermute(buffer, axis, xor_pairs(axis, mask))
        pair = jnp.stack([buffer, other])
        first = lax.dynamic_index_in_dim(pair, upper, axis=0, keepdims=False)
        second = lax.dynamic_index_in_dim(pair, 1 - upper, axis=0, keepdims=False)
        buffer = jnp.concatenate([first, second], axis=0)
    out = []
    for g, start in zip(grads, offsets):
        count = -(-g.size // lanes)
        part = buffer[start : start + count].reshape(-1)[: g.size]
        out.append(part.reshape(g.shape))
    return tuple(out)


def solution(mesh):
    in_specs = (
        P(None, "sample", "slab", None),
        P(None, "sample", "slab", None),
        P(),
        P(),
        P(),
        P(),
        P(),
        P(),
    )
    out_specs = (P(None, "sample", "slab", None), P(), P(), P(), P(), P(), P())
    return jax.shard_map(
        per_device, mesh=mesh, in_specs=in_specs, out_specs=out_specs, check_vma=False
    )
```

```python
import functools

import jax
import jax.numpy as jnp
from jax import lax
from jax.experimental import pallas as pl
from jax.experimental.pallas import tpu as pltpu
from jax.sharding import PartitionSpec as P

SX = 32
CZ = 4


def with_halo(shard, sides, width):
    for axis, dim in sides:
        size, length = (lax.axis_size(axis), shard.shape[dim])
        up = [(i, (i + 1) % size) for i in range(size - 1)]
        down = [(j, i) for i, j in up]
        last = lax.slice_in_dim(shard, length - width, length, axis=dim)
        first = lax.slice_in_dim(shard, 0, width, axis=dim)
        before = lax.ppermute(last, axis, up)
        after = lax.ppermute(first, axis, down)
        shard = jnp.concatenate([before, shard, after], axis=dim)
    return shard


def silu_slope(values):
    sigmoid = jax.nn.sigmoid(values)
    return sigmoid * (1.0 + values * (1.0 - sigmoid))


def put_block(values, update, sample, depth_start):
    return lax.dynamic_update_slice(values, update, (0, sample, depth_start, 0))


def gather_taps(section, row_width):
    depth_len = section.shape[2] - 2
    plane_size = section.shape[3]
    flattened = jnp.pad(section, ((0, 0), (0, 0), (0, 0), (row_width + 1, row_width + 1)))
    column = lax.broadcasted_iota(jnp.int32, (1, 1, 1, plane_size), 3) % row_width
    left_mask = (column >= 1).astype(section.dtype)
    right_mask = (column <= row_width - 2).astype(section.dtype)
    pieces = []
    for tap_index in range(27):
        depth_start = tap_index // 9
        row_step = tap_index // 3 % 3 - 1
        col_step = tap_index % 3 - 1
        offset = row_width + 1 + row_step * row_width + col_step
        shifted = flattened[
            :, :, depth_start : depth_start + depth_len, offset : offset + plane_size
        ]
        if col_step < 0:
            shifted = shifted * left_mask
        elif col_step > 0:
            shifted = shifted * right_mask
        pieces.append(shifted)
    return jnp.concatenate(pieces, axis=0)


def apply_weight(patches, weight):
    flat_weight = weight.reshape(weight.shape[0] * weight.shape[1], weight.shape[2])
    return jnp.einsum("ko,kgzp->ogzp", flat_weight, patches, preferred_element_type=jnp.float32)


def weight_term(patches, grad_block, in_channels):
    summed = jnp.einsum("kgzp,ogzp->ko", patches, grad_block, preferred_element_type=jnp.float32)
    return summed.reshape(27, in_channels, grad_block.shape[0])


def pool_cells(values, row_width):
    channels, samples, depth_len, plane_size = values.shape
    row_count = plane_size // row_width
    grouped = values.reshape(
        channels, samples, depth_len // 2, 2, row_count // 2, 2, row_width // 2, 2
    )
    return grouped.mean(axis=(3, 5, 7)).reshape(channels, samples, depth_len // 2, plane_size // 4)


def spread_cells(values, coarse_width):
    channels, samples, depth_len, plane_size = values.shape
    row_count = plane_size // coarse_width
    grouped = values.reshape(channels, samples, depth_len, 1, row_count, 1, coarse_width, 1)
    grouped = jnp.broadcast_to(
        grouped, (channels, samples, depth_len, 2, row_count, 2, coarse_width, 2)
    )
    return grouped.reshape(channels, samples, 2 * depth_len, 4 * plane_size) * 0.125


def forward_layer(padded, weight, bias_values, row_width, depth_block, pooled_out):
    out_channels = weight.shape[2]
    samples, depth_total, plane_size = (padded.shape[1], padded.shape[2] - 2, padded.shape[3])
    per_sample = depth_total // depth_block
    pre_buffer = jnp.zeros((out_channels, samples, depth_total, plane_size), jnp.bfloat16)
    if pooled_out:
        out_buffer = jnp.zeros(
            (out_channels, samples, depth_total // 2, plane_size // 4), jnp.bfloat16
        )
    else:
        out_buffer = jnp.zeros_like(pre_buffer)

    def forward_block_step(block_index, buffers):
        sample = block_index // per_sample
        depth_start = block_index % per_sample * depth_block
        pre_values = (
            apply_weight(gather_taps(padded, row_width), weight) + bias_values[:, None, None, None]
        ).astype(jnp.bfloat16)
        activated = jax.nn.silu(pre_values.astype(jnp.float32))
        if pooled_out:
            result = put_block(
                buffers[1],
                pool_cells(activated, row_width).astype(jnp.bfloat16),
                sample,
                depth_start // 2,
            )
        else:
            result = put_block(buffers[1], activated.astype(jnp.bfloat16), sample, depth_start)
        return (put_block(buffers[0], pre_values, sample, depth_start), result)

    return lax.fori_loop(0, samples * per_sample, forward_block_step, (pre_buffer, out_buffer))


def weight_grads(padded, delta_values, row_width, depth_block, weight):
    samples, depth_total = (delta_values.shape[1], delta_values.shape[2])
    per_sample = depth_total // depth_block
    in_channels = weight.shape[1]

    def weight_block_step(block_index, summed):
        return summed + weight_term(gather_taps(padded, row_width), delta_values, in_channels)

    return lax.fori_loop(
        0, samples * per_sample, weight_block_step, jnp.zeros(weight.shape, jnp.float32)
    )


def data_grads(padded, flipped, row_width, depth_block):
    out_channels = flipped.shape[2]
    samples, depth_total, plane_size = (padded.shape[1], padded.shape[2] - 2, padded.shape[3])
    per_sample = depth_total // depth_block
    out_buffer = jnp.zeros((out_channels, samples, depth_total, plane_size), jnp.bfloat16)

    def data_block_step(block_index, buffer_now):
        sample = block_index // per_sample
        depth_start = block_index % per_sample * depth_block
        result = apply_weight(gather_taps(padded, row_width), flipped).astype(jnp.bfloat16)
        return put_block(buffer_now, result, sample, depth_start)

    return lax.fori_loop(0, samples * per_sample, data_block_step, out_buffer)


def parity_pool(values):
    c, n, z, parities, size = values.shape
    return values.reshape(c, n, z // 2, 2 * parities, size).mean(axis=3)

def parity_spread(values):
    c, n, z, size = values.shape
    grouped = jnp.broadcast_to(values[:, :, :, None, None, :], (c, n, z, 2, 4, size))
    return grouped.reshape(c, n, 2 * z, 4, size) * 0.125


def parity_permutation(row_width, chunk=128):
    lane = jnp.arange(chunk)
    yy, x = lane // row_width, lane % row_width
    target = ((yy % 2) * 2 + x % 2) * (chunk // 4) + (yy // 2) * (row_width // 2) + x // 2
    return (target[:, None] == jnp.arange(chunk)[None, :]).astype(jnp.bfloat16)

def _parity_kernel(coarse_width, channels, src_ref, perm_ref, w_ref, b_ref, out_ref, shifted_ref, sub_ref):
    rows_total, plane = src_ref.shape
    depth = rows_total // channels
    chunk = perm_ref.shape[0]
    quarter = chunk // 4
    for g in range(plane // chunk):
        moved = jnp.dot(src_ref[:, g * chunk : (g + 1) * chunk], perm_ref[...], preferred_element_type=jnp.float32)
        for s in range(4):
            sub_ref[s, :, g * quarter : (g + 1) * quarter] = moved[:, s * quarter : (s + 1) * quarter]
    size = plane // 4
    lane = lax.broadcasted_iota(jnp.int32, (channels, size), 1)
    row = lane // coarse_width
    col = lane % coarse_width
    rows = size // coarse_width
    for source_plane in range(depth):
        cache = {}
        for a in range(2):
            for b in range(2):
                for shift_index in range(9):
                    row_sum = a + shift_index // 3 - 1
                    col_sum = b + shift_index % 3 - 1
                    key = (row_sum % 2, col_sum % 2, row_sum // 2, col_sum // 2)
                    if key not in cache:
                        source, row_step, col_step = key[0] * 2 + key[1], key[2], key[3]
                        values = sub_ref[source, source_plane * channels : (source_plane + 1) * channels, :]
                        step = row_step * coarse_width + col_step
                        if step != 0:
                            values = pltpu.roll(values, (-step) % size, 1)
                        valid = (
                            (row + row_step >= 0) & (row + row_step < rows)
                            & (col + col_step >= 0) & (col + col_step < coarse_width)
                        )
                        cache[key] = jnp.where(valid, values, 0.0).astype(shifted_ref.dtype)
                    shifted_ref[source_plane, a * 2 + b, shift_index * channels : (shift_index + 1) * channels, :] = cache[key]
    for z in range(out_ref.shape[1]):
        for parity in range(4):
            summed = b_ref[...] + jnp.zeros((out_ref.shape[0], size), jnp.float32)
            for dz in range(3):
                summed = summed + jnp.dot(
                    w_ref[dz], shifted_ref[z + dz, parity], preferred_element_type=jnp.float32
                )
            out_ref[:, z, parity, :] = summed.astype(out_ref.dtype)

def parity_conv_forward(padded, weight, bias_values, row_width):
    channels, depth, plane = padded.shape
    out_channels = weight.shape[2]
    per_depth = weight.reshape(3, 9 * channels, out_channels).transpose(0, 2, 1)
    by_plane = padded.transpose(1, 0, 2).reshape(depth * channels, plane)
    return pl.pallas_call(
        functools.partial(_parity_kernel, row_width // 2, channels),
        out_shape=(
            jax.ShapeDtypeStruct((out_channels, depth - 2, 4, plane // 4), jnp.bfloat16),
            jax.ShapeDtypeStruct((depth, 4, 9 * channels, plane // 4), jnp.bfloat16),
        ),
        scratch_shapes=[pltpu.VMEM((4, depth * channels, plane // 4), jnp.float32)],
    )(by_plane, parity_permutation(row_width), per_depth, bias_values.reshape(out_channels, 1))


def parity_weight_grad(shifted, delta):
    depth_len = delta.shape[1]
    per_depth = [
        jnp.einsum(
            "zpkq,ozpq->ko", shifted[dz : dz + depth_len], delta, preferred_element_type=jnp.float32
        )
        for dz in range(3)
    ]
    return jnp.stack(per_depth).reshape(27, shifted.shape[2] // 9, delta.shape[0])


def bias_sum(delta_values):
    return jnp.sum(delta_values, axis=(1, 2, 3), dtype=jnp.float32)


def per_device(volume, cotangent, w_first, b_first, w_second, b_second, w_third, b_third):
    flipped_second = jnp.flip(w_second, 0).transpose(0, 2, 1)
    flipped_third = jnp.flip(w_third, 0).transpose(0, 2, 1)
    volume_padded = with_halo(volume, (("slab", 2),), 1)
    first_layer = [
        parity_conv_forward(volume_padded[:, s], w_first, b_first, SX)
        for s in range(volume_padded.shape[1])
    ]
    first_pre = jnp.stack([pre for pre, _ in first_layer], axis=1)
    first_pooled = parity_pool(jax.nn.silu(first_pre.astype(jnp.float32))).astype(jnp.bfloat16)
    first_padded = with_halo(first_pooled, (("slab", 2),), 1)
    second_pre, second_pooled = forward_layer(
        first_padded, w_second, b_second, SX // 2, CZ // 2, True
    )
    coarse_depth = second_pooled.shape[2]
    third_padded = with_halo(second_pooled, (("slab", 2),), 1)
    third_pre, features = forward_layer(
        third_padded, w_third, b_third, SX // 4, coarse_depth, False
    )
    third_delta = (
        cotangent.astype(jnp.float32) * silu_slope(third_pre.astype(jnp.float32))
    ).astype(jnp.bfloat16)
    kernel_third = weight_grads(third_padded, third_delta, SX // 4, coarse_depth, w_third)
    bias_third = bias_sum(third_delta)
    delta_window = with_halo(third_delta, (("slab", 2),), 1)
    second_back = data_grads(delta_window, flipped_third, SX // 4, coarse_depth)
    second_delta = (
        spread_cells(second_back.astype(jnp.float32), SX // 4)
        * silu_slope(second_pre.astype(jnp.float32))
    ).astype(jnp.bfloat16)
    kernel_second = weight_grads(first_padded, second_delta, SX // 2, CZ // 2, w_second)
    bias_second = bias_sum(second_delta)
    delta_padded = with_halo(second_delta, (("slab", 2),), 1)
    first_back = data_grads(delta_padded, flipped_second, SX // 2, CZ // 2)
    first_delta = (
        parity_spread(first_back.astype(jnp.float32)) * silu_slope(first_pre.astype(jnp.float32))
    ).astype(jnp.bfloat16)
    kernel_first = sum(
        parity_weight_grad(shifted, first_delta[:, s])
        for s, (_, shifted) in enumerate(first_layer)
    )
    bias_first = jnp.sum(first_delta, axis=(1, 2, 3, 4), dtype=jnp.float32)
    weights = all_reduce_rows(
        (kernel_third, kernel_second, kernel_first, bias_third, bias_second, bias_first)
    )
    kernel_third, kernel_second, kernel_first, bias_third, bias_second, bias_first = weights
    return (
        features,
        kernel_first,
        bias_first,
        kernel_second,
        bias_second,
        kernel_third,
        bias_third,
    )


def xor_pairs(axis, mask):
    return [(i, i ^ mask) for i in range(lax.axis_size(axis))]


def all_reduce_rows(grads, halving_steps=4, lanes=128):
    steps = []
    for axis in ("sample", "slab"):
        mask = 1
        while mask < lax.axis_size(axis):
            steps.append((axis, mask))
            mask *= 2
    pieces, offsets = [], []
    rows = 0
    for g in grads:
        count = -(-g.size // lanes)
        flat = g.reshape(-1)
        flat = jnp.pad(flat, (0, count * lanes - g.size))
        pieces.append(flat.reshape(count, lanes))
        offsets.append(rows)
        rows += count
    block = 8 << halving_steps
    total = -(-rows // block) * block
    if total > rows:
        pieces.append(jnp.zeros((total - rows, lanes), jnp.float32))
    buffer = jnp.concatenate(pieces, axis=0)
    kept = []
    for axis, mask in steps[:halving_steps]:
        half = buffer.shape[0] // 2
        upper = ((lax.axis_index(axis) // mask) % 2).astype(jnp.int32)
        send = lax.dynamic_slice_in_dim(buffer, (1 - upper) * half, half, axis=0)
        keep = lax.dynamic_slice_in_dim(buffer, upper * half, half, axis=0)
        buffer = keep + lax.ppermute(send, axis, xor_pairs(axis, mask))
        kept.append((axis, mask, upper))
    for axis, mask in steps[halving_steps:]:
        buffer = buffer + lax.ppermute(buffer, axis, xor_pairs(axis, mask))
    for axis, mask, upper in reversed(kept):
        other = lax.ppermute(buffer, axis, xor_pairs(axis, mask))
        pair = jnp.stack([buffer, other])
        first = lax.dynamic_index_in_dim(pair, upper, axis=0, keepdims=False)
        second = lax.dynamic_index_in_dim(pair, 1 - upper, axis=0, keepdims=False)
        buffer = jnp.concatenate([first, second], axis=0)
    out = []
    for g, start in zip(grads, offsets):
        count = -(-g.size // lanes)
        part = buffer[start : start + count].reshape(-1)[: g.size]
        out.append(part.reshape(g.shape))
    return tuple(out)


def solution(mesh):
    in_specs = (
        P(None, "sample", "slab", None),
        P(None, "sample", "slab", None),
        P(),
        P(),
        P(),
        P(),
        P(),
        P(),
    )
    out_specs = (P(None, "sample", "slab", None), P(), P(), P(), P(), P(), P())
    return jax.shard_map(
        per_device, mesh=mesh, in_specs=in_specs, out_specs=out_specs, check_vma=False
    )
```

```python
import functools

import jax
import jax.numpy as jnp
from jax import lax
from jax.experimental import pallas as pl
from jax.experimental.pallas import tpu as pltpu
from jax.sharding import PartitionSpec as P

SX = 32
CZ = 4


def with_halo(shard, sides, width):
    for axis, dim in sides:
        size, length = (lax.axis_size(axis), shard.shape[dim])
        up = [(i, (i + 1) % size) for i in range(size - 1)]
        down = [(j, i) for i, j in up]
        last = lax.slice_in_dim(shard, length - width, length, axis=dim)
        first = lax.slice_in_dim(shard, 0, width, axis=dim)
        before = lax.ppermute(last, axis, up)
        after = lax.ppermute(first, axis, down)
        shard = jnp.concatenate([before, shard, after], axis=dim)
    return shard


def silu_slope(values):
    sigmoid = jax.nn.sigmoid(values)
    return sigmoid * (1.0 + values * (1.0 - sigmoid))


def put_block(values, update, sample, depth_start):
    return lax.dynamic_update_slice(values, update, (0, sample, depth_start, 0))


def gather_taps(section, row_width):
    depth_len = section.shape[2] - 2
    plane_size = section.shape[3]
    flattened = jnp.pad(section, ((0, 0), (0, 0), (0, 0), (row_width + 1, row_width + 1)))
    column = lax.broadcasted_iota(jnp.int32, (1, 1, 1, plane_size), 3) % row_width
    left_mask = (column >= 1).astype(section.dtype)
    right_mask = (column <= row_width - 2).astype(section.dtype)
    pieces = []
    for tap_index in range(27):
        depth_start = tap_index // 9
        row_step = tap_index // 3 % 3 - 1
        col_step = tap_index % 3 - 1
        offset = row_width + 1 + row_step * row_width + col_step
        shifted = flattened[
            :, :, depth_start : depth_start + depth_len, offset : offset + plane_size
        ]
        if col_step < 0:
            shifted = shifted * left_mask
        elif col_step > 0:
            shifted = shifted * right_mask
        pieces.append(shifted)
    return jnp.concatenate(pieces, axis=0)


def apply_weight(patches, weight):
    flat_weight = weight.reshape(weight.shape[0] * weight.shape[1], weight.shape[2])
    return jnp.einsum("ko,kgzp->ogzp", flat_weight, patches, preferred_element_type=jnp.float32)


def weight_term(patches, grad_block, in_channels):
    summed = jnp.einsum("kgzp,ogzp->ko", patches, grad_block, preferred_element_type=jnp.float32)
    return summed.reshape(27, in_channels, grad_block.shape[0])


def pool_cells(values, row_width):
    channels, samples, depth_len, plane_size = values.shape
    row_count = plane_size // row_width
    grouped = values.reshape(
        channels, samples, depth_len // 2, 2, row_count // 2, 2, row_width // 2, 2
    )
    return grouped.mean(axis=(3, 5, 7)).reshape(channels, samples, depth_len // 2, plane_size // 4)


def spread_cells(values, coarse_width):
    channels, samples, depth_len, plane_size = values.shape
    row_count = plane_size // coarse_width
    grouped = values.reshape(channels, samples, depth_len, 1, row_count, 1, coarse_width, 1)
    grouped = jnp.broadcast_to(
        grouped, (channels, samples, depth_len, 2, row_count, 2, coarse_width, 2)
    )
    return grouped.reshape(channels, samples, 2 * depth_len, 4 * plane_size) * 0.125


def forward_layer(padded, weight, bias_values, row_width, depth_block, pooled_out):
    out_channels = weight.shape[2]
    samples, depth_total, plane_size = (padded.shape[1], padded.shape[2] - 2, padded.shape[3])
    per_sample = depth_total // depth_block
    pre_buffer = jnp.zeros((out_channels, samples, depth_total, plane_size), jnp.bfloat16)
    if pooled_out:
        out_buffer = jnp.zeros(
            (out_channels, samples, depth_total // 2, plane_size // 4), jnp.bfloat16
        )
    else:
        out_buffer = jnp.zeros_like(pre_buffer)

    def forward_block_step(block_index, buffers):
        sample = block_index // per_sample
        depth_start = block_index % per_sample * depth_block
        pre_values = (
            apply_weight(gather_taps(padded, row_width), weight) + bias_values[:, None, None, None]
        ).astype(jnp.bfloat16)
        activated = jax.nn.silu(pre_values.astype(jnp.float32))
        if pooled_out:
            result = put_block(
                buffers[1],
                pool_cells(activated, row_width).astype(jnp.bfloat16),
                sample,
                depth_start // 2,
            )
        else:
            result = put_block(buffers[1], activated.astype(jnp.bfloat16), sample, depth_start)
        return (put_block(buffers[0], pre_values, sample, depth_start), result)

    return lax.fori_loop(0, samples * per_sample, forward_block_step, (pre_buffer, out_buffer))


def weight_grads(padded, delta_values, row_width, depth_block, weight):
    samples, depth_total = (delta_values.shape[1], delta_values.shape[2])
    per_sample = depth_total // depth_block
    in_channels = weight.shape[1]

    def weight_block_step(block_index, summed):
        return summed + weight_term(gather_taps(padded, row_width), delta_values, in_channels)

    return lax.fori_loop(
        0, samples * per_sample, weight_block_step, jnp.zeros(weight.shape, jnp.float32)
    )


def data_grads(padded, flipped, row_width, depth_block):
    out_channels = flipped.shape[2]
    samples, depth_total, plane_size = (padded.shape[1], padded.shape[2] - 2, padded.shape[3])
    per_sample = depth_total // depth_block
    out_buffer = jnp.zeros((out_channels, samples, depth_total, plane_size), jnp.bfloat16)

    def data_block_step(block_index, buffer_now):
        sample = block_index // per_sample
        depth_start = block_index % per_sample * depth_block
        result = apply_weight(gather_taps(padded, row_width), flipped).astype(jnp.bfloat16)
        return put_block(buffer_now, result, sample, depth_start)

    return lax.fori_loop(0, samples * per_sample, data_block_step, out_buffer)


def parity_pool(values):
    c, n, z, parities, size = values.shape
    return values.reshape(c, n, z // 2, 2 * parities, size).mean(axis=3)

def parity_spread(values):
    c, n, z, size = values.shape
    grouped = jnp.broadcast_to(values[:, :, :, None, None, :], (c, n, z, 2, 4, size))
    return grouped.reshape(c, n, 2 * z, 4, size) * 0.125


def parity_permutation(row_width, chunk=128):
    lane = jnp.arange(chunk)
    yy, x = lane // row_width, lane % row_width
    target = ((yy % 2) * 2 + x % 2) * (chunk // 4) + (yy // 2) * (row_width // 2) + x // 2
    return (target[:, None] == jnp.arange(chunk)[None, :]).astype(jnp.bfloat16)

def _parity_kernel(coarse_width, channels, src_ref, perm_ref, w_ref, b_ref, out_ref, shifted_ref, sub_ref):
    rows_total, plane = src_ref.shape
    depth = rows_total // channels
    chunk = perm_ref.shape[0]
    quarter = chunk // 4
    for g in range(plane // chunk):
        moved = jnp.dot(src_ref[:, g * chunk : (g + 1) * chunk], perm_ref[...], preferred_element_type=jnp.float32)
        for s in range(4):
            sub_ref[s, :, g * quarter : (g + 1) * quarter] = moved[:, s * quarter : (s + 1) * quarter]
    size = plane // 4
    lane = lax.broadcasted_iota(jnp.int32, (channels, size), 1)
    row = lane // coarse_width
    col = lane % coarse_width
    rows = size // coarse_width
    for source_plane in range(depth):
        cache = {}
        for a in range(2):
            for b in range(2):
                for shift_index in range(9):
                    row_sum = a + shift_index // 3 - 1
                    col_sum = b + shift_index % 3 - 1
                    key = (row_sum % 2, col_sum % 2, row_sum // 2, col_sum // 2)
                    if key not in cache:
                        source, row_step, col_step = key[0] * 2 + key[1], key[2], key[3]
                        values = sub_ref[source, source_plane * channels : (source_plane + 1) * channels, :]
                        step = row_step * coarse_width + col_step
                        if step != 0:
                            values = pltpu.roll(values, (-step) % size, 1)
                        valid = (
                            (row + row_step >= 0) & (row + row_step < rows)
                            & (col + col_step >= 0) & (col + col_step < coarse_width)
                        )
                        cache[key] = jnp.where(valid, values, 0.0).astype(shifted_ref.dtype)
                    shifted_ref[source_plane, a * 2 + b, shift_index * channels : (shift_index + 1) * channels, :] = cache[key]
    for z in range(out_ref.shape[1]):
        for parity in range(4):
            summed = b_ref[...] + jnp.zeros((out_ref.shape[0], size), jnp.float32)
            for dz in range(3):
                summed = summed + jnp.dot(
                    w_ref[dz], shifted_ref[z + dz, parity], preferred_element_type=jnp.float32
                )
            out_ref[:, z, parity, :] = summed.astype(out_ref.dtype)

def parity_conv_forward(padded, weight, bias_values, row_width):
    channels, depth, plane = padded.shape
    out_channels = weight.shape[2]
    per_depth = weight.reshape(3, 9 * channels, out_channels).transpose(0, 2, 1)
    by_plane = padded.transpose(1, 0, 2).reshape(depth * channels, plane)
    return pl.pallas_call(
        functools.partial(_parity_kernel, row_width // 2, channels),
        out_shape=(
            jax.ShapeDtypeStruct((out_channels, depth - 2, 4, plane // 4), jnp.bfloat16),
            jax.ShapeDtypeStruct((depth, 4, 9 * channels, plane // 4), jnp.bfloat16),
        ),
        scratch_shapes=[pltpu.VMEM((4, depth * channels, plane // 4), jnp.float32)],
    )(by_plane, parity_permutation(row_width), per_depth, bias_values.reshape(out_channels, 1))


def parity_weight_grad(shifted, delta):
    depth_len = delta.shape[1]
    per_depth = [
        jnp.einsum(
            "zpkq,ozpq->ko", shifted[dz : dz + depth_len], delta, preferred_element_type=jnp.float32
        )
        for dz in range(3)
    ]
    return jnp.stack(per_depth).reshape(27, shifted.shape[2] // 9, delta.shape[0])


def bias_sum(delta_values):
    return jnp.sum(delta_values, axis=(1, 2, 3), dtype=jnp.float32)


def per_device(volume, cotangent, w_first, b_first, w_second, b_second, w_third, b_third):
    flipped_second = jnp.flip(w_second, 0).transpose(0, 2, 1)
    flipped_third = jnp.flip(w_third, 0).transpose(0, 2, 1)
    volume_padded = with_halo(volume, (("slab", 2),), 1)
    first_layer = [
        parity_conv_forward(volume_padded[:, s], w_first, b_first, SX)
        for s in range(volume_padded.shape[1])
    ]
    first_pre = jnp.stack([pre for pre, _ in first_layer], axis=1)
    first_pooled = parity_pool(jax.nn.silu(first_pre.astype(jnp.float32))).astype(jnp.bfloat16)
    first_padded = with_halo(first_pooled, (("slab", 2),), 1)
    second_pre, second_pooled = forward_layer(
        first_padded, w_second, b_second, SX // 2, CZ // 2, True
    )
    coarse_depth = second_pooled.shape[2]
    third_padded = with_halo(second_pooled, (("slab", 2),), 1)
    third_pre, features = forward_layer(
        third_padded, w_third, b_third, SX // 4, coarse_depth, False
    )
    third_delta = (
        cotangent.astype(jnp.float32) * silu_slope(third_pre.astype(jnp.float32))
    ).astype(jnp.bfloat16)
    kernel_third = weight_grads(third_padded, third_delta, SX // 4, coarse_depth, w_third)
    bias_third = bias_sum(third_delta)
    delta_window = with_halo(third_delta, (("slab", 2),), 1)
    second_back = data_grads(delta_window, flipped_third, SX // 4, coarse_depth)
    second_delta = (
        spread_cells(second_back.astype(jnp.float32), SX // 4)
        * silu_slope(second_pre.astype(jnp.float32))
    ).astype(jnp.bfloat16)
    kernel_second = weight_grads(first_padded, second_delta, SX // 2, CZ // 2, w_second)
    bias_second = bias_sum(second_delta)
    delta_padded = with_halo(second_delta, (("slab", 2),), 1)
    first_back = data_grads(delta_padded, flipped_second, SX // 2, CZ // 2)
    first_delta = (
        parity_spread(first_back.astype(jnp.float32)) * silu_slope(first_pre.astype(jnp.float32))
    ).astype(jnp.bfloat16)
    kernel_first = sum(
        parity_weight_grad(shifted, first_delta[:, s])
        for s, (_, shifted) in enumerate(first_layer)
    )
    bias_first = jnp.sum(first_delta, axis=(1, 2, 3, 4), dtype=jnp.float32)
    weights = all_reduce_rows(
        (kernel_third, kernel_second, kernel_first, bias_third, bias_second, bias_first)
    )
    kernel_third, kernel_second, kernel_first, bias_third, bias_second, bias_first = weights
    return (
        features,
        kernel_first,
        bias_first,
        kernel_second,
        bias_second,
        kernel_third,
        bias_third,
    )


def xor_pairs(axis, mask):
    return [(i, i ^ mask) for i in range(lax.axis_size(axis))]


def all_reduce_rows(grads, halving_steps=4, lanes=128):
    steps = []
    for axis in ("sample", "slab"):
        mask = 1
        while mask < lax.axis_size(axis):
            steps.append((axis, mask))
            mask *= 2
    near = {("sample", 1), ("sample", 2), ("sample", 8), ("slab", 1)}
    steps.sort(key=lambda step: step not in near)
    pieces, offsets = [], []
    rows = 0
    for g in grads:
        count = -(-g.size // lanes)
        flat = g.reshape(-1)
        flat = jnp.pad(flat, (0, count * lanes - g.size))
        pieces.append(flat.reshape(count, lanes))
        offsets.append(rows)
        rows += count
    block = 8 << halving_steps
    total = -(-rows // block) * block
    if total > rows:
        pieces.append(jnp.zeros((total - rows, lanes), jnp.float32))
    buffer = jnp.concatenate(pieces, axis=0)
    kept = []
    for axis, mask in steps[:halving_steps]:
        half = buffer.shape[0] // 2
        upper = ((lax.axis_index(axis) // mask) % 2).astype(jnp.int32)
        send = lax.dynamic_slice_in_dim(buffer, (1 - upper) * half, half, axis=0)
        keep = lax.dynamic_slice_in_dim(buffer, upper * half, half, axis=0)
        buffer = keep + lax.ppermute(send, axis, xor_pairs(axis, mask))
        kept.append((axis, mask, upper))
    for axis, mask in steps[halving_steps:]:
        buffer = buffer + lax.ppermute(buffer, axis, xor_pairs(axis, mask))
    for axis, mask, upper in reversed(kept):
        other = lax.ppermute(buffer, axis, xor_pairs(axis, mask))
        pair = jnp.stack([buffer, other])
        first = lax.dynamic_index_in_dim(pair, upper, axis=0, keepdims=False)
        second = lax.dynamic_index_in_dim(pair, 1 - upper, axis=0, keepdims=False)
        buffer = jnp.concatenate([first, second], axis=0)
    out = []
    for g, start in zip(grads, offsets):
        count = -(-g.size // lanes)
        part = buffer[start : start + count].reshape(-1)[: g.size]
        out.append(part.reshape(g.shape))
    return tuple(out)


def solution(mesh):
    in_specs = (
        P(None, "sample", "slab", None),
        P(None, "sample", "slab", None),
        P(),
        P(),
        P(),
        P(),
        P(),
        P(),
    )
    out_specs = (P(None, "sample", "slab", None), P(), P(), P(), P(), P(), P())
    return jax.shard_map(
        per_device, mesh=mesh, in_specs=in_specs, out_specs=out_specs, check_vma=False
    )
```
